512 devices in a mesh: chain: 64 (over y, z), sector: 8 (over x, core).
Axes of the slice: x: 4, y: 8, z: 8, core: 2. Of those that a mesh axis runs over, the one named last changes fastest.
Arguments:
- psi_start: bfloat16 [64, 16, 128, 128], P('chain', 'sector'), may hold values from -6 to 6
- left_terms: bfloat16 [64, 2, 16, 128, 128], P('chain', None, 'sector'), may hold values from -0.5 to 0.5
- left_rate: float32 [64, 2, 16, 128], P('chain', None, 'sector'), may hold values from 0.004 to 0.5
- right_terms: bfloat16 [64, 2, 16, 128, 128], P('chain', None, 'sector'), may hold values from -0.5 to 0.5
- right_rate: float32 [64, 2, 16, 128], P('chain', None, 'sector'), may hold values from 0.004 to 0.5
- term_left: int32 [12], replicated, may hold values from 0 to 1
- term_right: int32 [12], replicated, may hold values from 0 to 1
- term_shift: int32 [12], replicated, may hold values from -2 to 2
- term_coef: float32 [12], replicated, may hold values from 0.5 to 1.5
Outputs:
- psi_final: float32 [64, 16, 128, 128], P('chain', 'sector')
- rayleigh_cos: float32 [64], P('chain')
The draws below stay inside these ranges and needn't reach their ends.
All inputs are finite; a program needn't handle non-finite values.
Results may differ from the reference program's by a relative error of at most 0.0058.
Values may be sent and summed in bfloat16 or wider, within the bound.
No kernel may reach another device: no remote copies, remote signals or barrier semaphores. Data moves between devices by JAX's collectives and lax.ppermute only.
A program may use at most 128 MiB of HBM per device.

```python
import math
import jax
import jax.numpy as jnp
from jax import lax

SB = 128
ENV = 2
TERMS = 12
ITERS = 4
SECTORS = 16
GROUPS = 64


def set_ends(values, stream_key, smallest, top_value):
    extent = values.shape
    index_at = [jax.random.randint(jax.random.fold_in(stream_key, axis), (), 0, extent[axis]) for axis in range(len(extent))]
    values = values.at[tuple(index_at)].set(smallest)
    longest = extent.index(max(extent))
    index_at[longest] = (index_at[longest] + 1) % extent[longest]
    return values.at[tuple(index_at)].set(top_value)


def shard_levels(rng, shape, cuts, low, top_value):
    gain = 1.0
    for dim, parts in cuts:
        steps = jax.random.uniform(jax.random.fold_in(jax.random.fold_in(rng, 6), dim), (parts,), jnp.float32, low / len(cuts), top_value / len(cuts))
        gain = gain * jnp.repeat(jnp.exp(steps), shape[dim] // parts).reshape((-1,) + (1,) * (len(shape) - 1 - dim))
    return gain


def bell_draw(stream_key, extent, spread, limit, shards=(), held_as=jnp.bfloat16):
    factor_of = shard_levels(stream_key, extent, shards, -0.22, 0.18) if shards else 1.0
    drawn = jax.random.normal(stream_key, extent, jnp.float32) * spread * factor_of
    return jnp.minimum(jnp.maximum(drawn, -limit), limit).astype(held_as)


def setup_inputs(seed: int = 0) -> dict:
    key_of = jax.random.split(jax.random.key(seed), 10)
    return {
        "psi_start": bell_draw(key_of[0], (GROUPS, SECTORS, SB, SB), 1.0, 6.0, ((0, 64), (1, 8))),
        "left_terms": bell_draw(key_of[1], (GROUPS, ENV, SECTORS, SB, SB), SB ** -0.5, 0.5, ((0, 64), (2, 8))),
        "left_rate": jnp.clip(jnp.exp(math.log(0.5) - 4.828314 * jax.random.uniform(key_of[2], (GROUPS, ENV, SECTORS, SB), jnp.float32) ** shard_levels(key_of[2], (GROUPS, ENV, SECTORS, SB), ((0, 64), (2, 8)), -0.2, 0.2)), 0.004, 0.5),
        "right_terms": bell_draw(key_of[3], (GROUPS, ENV, SECTORS, SB, SB), SB ** -0.5, 0.5, ((0, 64), (2, 8))),
        "right_rate": jnp.clip(jnp.exp(math.log(0.5) - 4.828314 * jax.random.uniform(key_of[4], (GROUPS, ENV, SECTORS, SB), jnp.float32) ** shard_levels(key_of[4], (GROUPS, ENV, SECTORS, SB), ((0, 64), (2, 8)), -0.2, 0.2)), 0.004, 0.5),
        "term_left": set_ends(jax.random.randint(key_of[5], (TERMS,), 0, ENV), jax.random.fold_in(key_of[5], 1), 0, ENV - 1).astype(jnp.int32),
        "term_right": set_ends(jax.random.randint(key_of[6], (TERMS,), 0, ENV), jax.random.fold_in(key_of[6], 1), 0, ENV - 1).astype(jnp.int32),
        "term_shift": set_ends(jax.random.randint(key_of[7], (TERMS,), -2, 3), jax.random.fold_in(key_of[7], 1), -2, 2).astype(jnp.int32),
        "term_coef": jnp.clip(jax.random.uniform(key_of[8], (TERMS,), jnp.float32, 0.5, 1.5), 0.5, 1.5),
    }


epsilon = 1e-06

def environments(terms, rate, backward):

    def advance(carry, inputs):
        decay_rate, source = inputs
        env_now = jnp.exp(-decay_rate)[..., None] * carry + source.astype(jnp.float32)
        return (env_now, env_now.astype(jnp.bfloat16))
    start = jnp.zeros(terms.shape[1:], jnp.float32)
    final_env, stacked = lax.scan(advance, start, (rate, terms), reverse=backward)
    return stacked

def solve_group(psi_start, left_env, right_env, term_left, term_right, term_shift, term_coef):
    entries = psi_start.size

    def apply_terms(vector):
        rounded = vector.astype(jnp.bfloat16)
        zeros_rim = jnp.zeros((2,) + rounded.shape[1:], jnp.bfloat16)
        padded = jnp.concatenate([zeros_rim, rounded, zeros_rim], axis=0)

        def add_term(term_index, running):
            moved_block = lax.dynamic_slice_in_dim(padded, (term_shift[term_index] + 2).astype(jnp.int32), rounded.shape[0], 0)
            left_sel = lax.dynamic_index_in_dim(left_env, term_left[term_index].astype(jnp.int32), 0, keepdims=False)
            right_sel = lax.dynamic_index_in_dim(right_env, term_right[term_index].astype(jnp.int32), 0, keepdims=False)
            left_product = jnp.einsum('sim,smj->sij', left_sel.astype(jnp.float32), moved_block.astype(jnp.float32)).astype(jnp.bfloat16)
            full_product = jnp.einsum('sim,sjm->sij', left_product.astype(jnp.float32), right_sel.astype(jnp.float32))
            return running + term_coef[term_index] * full_product
        return lax.fori_loop(0, term_coef.shape[0], add_term, jnp.zeros(vector.shape, jnp.float32))
    vector = psi_start.astype(jnp.float32)
    cosine = jnp.zeros((), jnp.float32)
    for iteration in range(ITERS):
        image = apply_terms(vector)
        self_dot = jnp.sum(vector * vector)
        cross_dot = jnp.sum(vector * image)
        image_dot = jnp.sum(image * image)
        rayleigh_now = cross_dot / self_dot
        step_size = 0.5 * jnp.sqrt(self_dot / (image_dot + epsilon))
        update = vector - step_size * (image - rayleigh_now * vector)
        vector = update * lax.rsqrt(jnp.sum(update * update) / entries + epsilon)
        cosine = cross_dot * lax.rsqrt(self_dot * (image_dot + epsilon))
    return (vector, cosine)

def reference(psi_start, left_terms, left_rate, right_terms, right_rate, term_left, term_right, term_shift, term_coef):
    left_all = environments(left_terms, left_rate, False)
    right_all = environments(right_terms, right_rate, True)

    def per_group(inputs):
        return solve_group(inputs[0], inputs[1], inputs[2], term_left, term_right, term_shift, term_coef)
    psi_final, rayleigh_cos = lax.map(per_group, (psi_start, left_all, right_all))
    return (psi_final, rayleigh_cos)
```

```python
import jax
import jax.numpy as jnp
from jax import lax
from jax.sharding import PartitionSpec as P

ITERS = 4
HALO = 2

epsilon = 1e-06


def chain_scan(decay, source, axis, reverse):
    count = lax.axis_size(axis)
    gain, total = decay, source
    distance = 1
    while distance < count:
        if reverse:
            pairs = [(i, i - distance) for i in range(distance, count)]
        else:
            pairs = [(i, i + distance) for i in range(count - distance)]
        got_gain, got_total = lax.ppermute((gain, total), axis, pairs)
        total = gain[..., None] * got_total + total
        if distance * 2 < count:
            gain = gain * got_gain
        distance *= 2
    return total


def body(
    psi_start,
    left_terms,
    left_rate,
    right_terms,
    right_rate,
    term_left,
    term_right,
    term_shift,
    term_coef,
):
    with jax.named_scope("psi_gather"):
        vector = lax.all_gather(psi_start[0], "sector", axis=0, tiled=True).astype(jnp.float32)
    with jax.named_scope("env_scan"):
        left_env = chain_scan(
            jnp.exp(-left_rate[0]), left_terms[0].astype(jnp.float32), "chain", False
        ).astype(jnp.bfloat16)
        right_env = chain_scan(
            jnp.exp(-right_rate[0]), right_terms[0].astype(jnp.float32), "chain", True
        ).astype(jnp.bfloat16)
    with jax.named_scope("env_gather"):
        left_env, right_env = lax.all_gather((left_env, right_env), "sector", axis=1, tiled=True)

    envs = left_env.shape[0]
    sectors = vector.shape[0]
    shifts = 2 * HALO + 1
    with jax.named_scope("term_table"):
        pick_right = (term_right[:, None] == jnp.arange(envs)[None]).astype(jnp.float32)
        pick_left = (term_left[:, None] == jnp.arange(envs)[None]).astype(jnp.float32)
        pick_shift = (term_shift[:, None] == jnp.arange(-HALO, HALO + 1)[None]).astype(jnp.float32)
        table = jnp.sum(
            term_coef[:, None, None, None]
            * pick_right[:, :, None, None]
            * pick_left[:, None, :, None]
            * pick_shift[:, None, None, :],
            axis=0,
        )

    entries = vector.size
    cosine = jnp.zeros((), jnp.float32)
    for iteration in range(ITERS):
        with jax.named_scope("apply_terms"):
            rounded = vector.astype(jnp.bfloat16)
            rim = jnp.zeros((HALO,) + rounded.shape[1:], jnp.bfloat16)
            padded = jnp.concatenate([rim, rounded, rim], axis=0)
            moved = jnp.stack([padded[t : t + sectors] for t in range(shifts)], axis=0)
            left_products = jnp.einsum(
                "esim,tsmj->etsij", left_env, moved, preferred_element_type=jnp.float32
            ).astype(jnp.bfloat16)
            summed = jnp.sum(
                table[:, :, :, None, None, None] * left_products[None].astype(jnp.float32),
                axis=(1, 2),
            )
            high = summed.astype(jnp.bfloat16)
            low = (summed - high.astype(jnp.float32)).astype(jnp.bfloat16)
            image = jnp.einsum(
                "rsim,rsjm->sij", high, right_env, preferred_element_type=jnp.float32
            ) + jnp.einsum("rsim,rsjm->sij", low, right_env, preferred_element_type=jnp.float32)
        with jax.named_scope("residual_step"):
            self_dot = jnp.sum(vector * vector)
            cross_dot = jnp.sum(vector * image)
            image_dot = jnp.sum(image * image)
            rayleigh_now = cross_dot / self_dot
            step_size = 0.5 * jnp.sqrt(self_dot / (image_dot + epsilon))
            update = vector - step_size * (image - rayleigh_now * vector)
            vector = update * lax.rsqrt(jnp.sum(update * update) / entries + epsilon)
            cosine = cross_dot * lax.rsqrt(self_dot * (image_dot + epsilon))
    local = psi_start.shape[1]
    mine = lax.dynamic_slice_in_dim(vector, lax.axis_index("sector") * local, local, 0)
    return (mine[None], jnp.reshape(cosine, (1,)))


def solution(mesh):
    placed = (
        P("chain", "sector", None, None),
        P("chain", None, "sector", None, None),
        P("chain", None, "sector", None),
        P("chain", None, "sector", None, None),
        P("chain", None, "sector", None),
        P(),
        P(),
        P(),
        P(),
    )
    return jax.shard_map(
        body,
        mesh=mesh,
        in_specs=placed,
        out_specs=(P("chain", "sector", None, None), P("chain")),
        check_vma=False,
    )
```

```python
import functools

import jax
import jax.numpy as jnp
from jax import lax
from jax.experimental import pallas as pl
from jax.experimental.pallas import tpu as pltpu
from jax.sharding import PartitionSpec as P

ITERS = 4
HALO = 2

epsilon = 1e-06


def chain_env(terms, rate, reverse):
    count = lax.axis_size("chain")
    shape = terms.shape
    width = shape[-1]
    rows = terms.size // width
    block = rows // count
    spread = lax.all_to_all(terms.reshape(count, block, width), "chain", 0, 0, tiled=True)
    speed = lax.all_to_all(rate.reshape(count, block), "chain", 0, 0, tiled=True)
    if reverse:
        spread, speed = spread[::-1], speed[::-1]
    total = jnp.cumsum(speed, axis=0)
    later = jnp.arange(count)[:, None, None] >= jnp.arange(count)[None, :, None]
    gap = jnp.where(later, total[:, None, :] - total[None, :, :], 0.0)
    weight = jnp.where(later, jnp.exp(-gap), 0.0)
    env = jnp.einsum(
        "ghp,hpc->gpc",
        weight,
        spread.astype(jnp.float32),
        precision=lax.Precision.HIGHEST,
        preferred_element_type=jnp.float32,
    )
    if reverse:
        env = env[::-1]
    back = lax.all_to_all(env.astype(jnp.bfloat16), "chain", 0, 0, tiled=True)
    return back.reshape(shape)


def _sum_all(a):
    return jnp.sum(jnp.sum(a, axis=0, keepdims=True), axis=1, keepdims=True)


def _fold(a):
    return jnp.sum(a.reshape(a.shape[0] // 8, 8, a.shape[1]), axis=0)


def iterate_kernel(
    table_ref, place_ref, psi_ref, left_ref, right_ref, out_ref, cos_ref, vec, image, padded
):
    sectors, side, _ = psi_ref.shape
    envs = left_ref.shape[0]
    shifts = 2 * HALO + 1
    entries = float(sectors * side * side)
    vec[...] = psi_ref[...].astype(jnp.float32)
    rim = jnp.zeros((HALO, side, side), jnp.bfloat16)
    padded[0:HALO] = rim
    padded[HALO + sectors : 2 * HALO + sectors] = rim
    nt = (((1,), (1,)), ((), ()))
    zero = jnp.zeros((8, side), jnp.float32)
    cosine = jnp.zeros((1, 1), jnp.float32)
    for iteration in range(ITERS):
        padded[HALO : HALO + sectors] = vec[...].astype(jnp.bfloat16)

        def apply(s, sums):
            lefts = left_ref[:, s].reshape(envs * side, side)
            parts = [jnp.zeros((side, side), jnp.float32) for _ in range(envs)]
            for t in range(shifts):
                prod = jnp.dot(lefts, padded[s + t], preferred_element_type=jnp.float32)
                prod = prod.astype(jnp.bfloat16).astype(jnp.float32)
                for e in range(envs):
                    piece = prod[e * side : (e + 1) * side]
                    for r in range(envs):
                        coef = table_ref[(r * envs + e) * shifts + t]
                        parts[r] = parts[r] + coef * piece
            y = jnp.zeros((side, side), jnp.float32)
            for r in range(envs):
                high = parts[r].astype(jnp.bfloat16)
                low = (parts[r] - high.astype(jnp.float32)).astype(jnp.bfloat16)
                rt = right_ref[r, s]
                y = y + lax.dot_general(high, rt, nt, preferred_element_type=jnp.float32)
                y = y + lax.dot_general(low, rt, nt, preferred_element_type=jnp.float32)
            image[s] = y
            x = vec[s]
            return (sums[0] + _fold(x * x), sums[1] + _fold(x * y), sums[2] + _fold(y * y))

        sx, sxy, sy = lax.fori_loop(0, sectors, apply, (zero, zero, zero))
        self_dot, cross_dot, image_dot = _sum_all(sx), _sum_all(sxy), _sum_all(sy)
        rayleigh_now = cross_dot / self_dot
        step_size = 0.5 * jnp.sqrt(self_dot / (image_dot + epsilon))

        def step(s, su):
            x = vec[s]
            u = x - step_size * (image[s] - rayleigh_now * x)
            vec[s] = u
            return su + _fold(u * u)

        su = _sum_all(lax.fori_loop(0, sectors, step, zero))
        scale = lax.rsqrt(su / entries + epsilon)

        def norm(s, carry):
            vec[s] = vec[s] * scale
            return carry

        lax.fori_loop(0, sectors, norm, 0)
        cosine = cross_dot * lax.rsqrt(self_dot * (image_dot + epsilon))
    local = out_ref.shape[0]
    out_ref[...] = vec[pl.ds(place_ref[0] * local, local)]
    cos_ref[...] = jnp.broadcast_to(cosine, cos_ref.shape)


def iterate(table, place, psi, left_env, right_env, local):
    sectors, side, _ = psi.shape
    smem = pl.BlockSpec(memory_space=pltpu.SMEM)
    vmem = pl.BlockSpec(memory_space=pltpu.VMEM)
    envs = left_env.shape[0]
    flops = ITERS * sectors * (2 * envs * (2 * HALO + 1) + 4 * envs) * 2 * side**3
    return pl.pallas_call(
        iterate_kernel,
        out_shape=(
            jax.ShapeDtypeStruct((local, side, side), jnp.float32),
            jax.ShapeDtypeStruct((8, 128), jnp.float32),
        ),
        in_specs=[smem, smem, vmem, vmem, vmem],
        out_specs=(vmem, vmem),
        scratch_shapes=[
            pltpu.VMEM((sectors, side, side), jnp.float32),
            pltpu.VMEM((sectors, side, side), jnp.float32),
            pltpu.VMEM((sectors + 2 * HALO, side, side), jnp.bfloat16),
        ],
        compiler_params=pltpu.CompilerParams(vmem_limit_bytes=48 * 1024 * 1024),
        cost_estimate=pl.CostEstimate(
            flops=flops, transcendentals=0, bytes_accessed=psi.size * 2 + 4 * left_env.size
        ),
    )(table, place, psi, left_env, right_env)


def body(
    psi_start,
    left_terms,
    left_rate,
    right_terms,
    right_rate,
    term_left,
    term_right,
    term_shift,
    term_coef,
):
    with jax.named_scope("psi_gather"):
        psi = lax.all_gather(psi_start[0], "sector", axis=0, tiled=True)
    with jax.named_scope("env_chain"):
        left_env = chain_env(left_terms[0], left_rate[0], False)
        right_env = chain_env(right_terms[0], right_rate[0], True)
    with jax.named_scope("env_gather"):
        left_env, right_env = lax.all_gather((left_env, right_env), "sector", axis=1, tiled=True)

    envs = left_env.shape[0]
    with jax.named_scope("term_table"):
        pick_right = (term_right[:, None] == jnp.arange(envs)[None]).astype(jnp.float32)
        pick_left = (term_left[:, None] == jnp.arange(envs)[None]).astype(jnp.float32)
        pick_shift = (term_shift[:, None] == jnp.arange(-HALO, HALO + 1)[None]).astype(jnp.float32)
        table = jnp.sum(
            term_coef[:, None, None, None]
            * pick_right[:, :, None, None]
            * pick_left[:, None, :, None]
            * pick_shift[:, None, None, :],
            axis=0,
        ).reshape(-1)
    local = psi_start.shape[1]
    place = jnp.reshape(lax.axis_index("sector"), (1,)).astype(jnp.int32)
    with jax.named_scope("iterations"):
        mine, cos = iterate(table, place, psi, left_env, right_env, local)
    return (mine[None], jnp.reshape(cos[0, 0], (1,)))


def solution(mesh):
    placed = (
        P("chain", "sector", None, None),
        P("chain", None, "sector", None, None),
        P("chain", None, "sector", None),
        P("chain", None, "sector", None, None),
        P("chain", None, "sector", None),
        P(),
        P(),
        P(),
        P(),
    )
    return jax.shard_map(
        body,
        mesh=mesh,
        in_specs=placed,
        out_specs=(P("chain", "sector", None, None), P("chain")),
        check_vma=False,
    )
```

```python
import functools

import jax
import jax.numpy as jnp
from jax import lax
from jax.experimental import pallas as pl
from jax.experimental.pallas import tpu as pltpu
from jax.sharding import PartitionSpec as P

ITERS = 4
HALO = 2

epsilon = 1e-06


def chain_envs(left_terms, left_rate, right_terms, right_rate):
    count = lax.axis_size("chain")
    shape = left_terms.shape
    width = shape[-1]
    block = left_terms.size // width // count
    packed = jnp.concatenate(
        [left_terms.reshape(count, block, width), right_terms.reshape(count, block, width)], axis=1
    )
    spread = lax.all_to_all(packed, "chain", 0, 0, tiled=True).astype(jnp.float32)
    rates = lax.all_gather(
        jnp.stack([left_rate.reshape(count, block), right_rate.reshape(count, block)]), "chain"
    )
    mine = lax.axis_index("chain")
    speed = lax.dynamic_index_in_dim(rates, mine, 2, keepdims=False)
    ahead = jnp.cumsum(speed[:, 0], axis=0)
    behind = jnp.cumsum(speed[::-1, 1], axis=0)[::-1]
    order = jnp.arange(count)
    later = (order[:, None] >= order[None, :])[:, :, None]
    earlier = (order[:, None] <= order[None, :])[:, :, None]
    forward = jnp.where(later, ahead[:, None, :] - ahead[None, :, :], 0.0)
    backward = jnp.where(earlier, behind[:, None, :] - behind[None, :, :], 0.0)
    weight = jnp.concatenate(
        [jnp.where(later, jnp.exp(-forward), 0.0), jnp.where(earlier, jnp.exp(-backward), 0.0)],
        axis=2,
    )
    env = jnp.einsum(
        "ghp,hpc->gpc",
        weight,
        spread,
        precision=lax.Precision.HIGHEST,
        preferred_element_type=jnp.float32,
    )
    back = lax.all_to_all(env.astype(jnp.bfloat16), "chain", 0, 0, tiled=True)
    return back[:, :block].reshape(shape), back[:, block:].reshape(shape)


def _sum_all(a):
    return jnp.sum(jnp.sum(a, axis=0, keepdims=True), axis=1, keepdims=True)


def _fold(a):
    return jnp.sum(a.reshape(a.shape[0] // 8, 8, a.shape[1]), axis=0)


def iterate_kernel(
    table_ref, place_ref, psi_ref, left_ref, right_ref, out_ref, cos_ref, vec, image, padded
):
    sectors, side, _ = psi_ref.shape
    envs = left_ref.shape[0]
    shifts = 2 * HALO + 1
    entries = float(sectors * side * side)
    vec[...] = psi_ref[...].astype(jnp.float32)
    rim = jnp.zeros((HALO, side, side), jnp.bfloat16)
    padded[0:HALO] = rim
    padded[HALO + sectors : 2 * HALO + sectors] = rim
    nt = (((1,), (1,)), ((), ()))
    zero = jnp.zeros((8, side), jnp.float32)
    cosine = jnp.zeros((1, 1), jnp.float32)
    for iteration in range(ITERS):
        padded[HALO : HALO + sectors] = vec[...].astype(jnp.bfloat16)

        def apply(s, sums):
            lefts = left_ref[:, s].reshape(envs * side, side)
            parts = [jnp.zeros((side, side), jnp.float32) for _ in range(envs)]
            for t in range(shifts):
                prod = jnp.dot(lefts, padded[s + t], preferred_element_type=jnp.float32)
                prod = prod.astype(jnp.bfloat16).astype(jnp.float32)
                for e in range(envs):
                    piece = prod[e * side : (e + 1) * side]
                    for r in range(envs):
                        coef = table_ref[(r * envs + e) * shifts + t]
                        parts[r] = parts[r] + coef * piece
            y = jnp.zeros((side, side), jnp.float32)
            for r in range(envs):
                high = parts[r].astype(jnp.bfloat16)
                low = (parts[r] - high.astype(jnp.float32)).astype(jnp.bfloat16)
                rt = right_ref[r, s]
                y = y + lax.dot_general(high, rt, nt, preferred_element_type=jnp.float32)
                y = y + lax.dot_general(low, rt, nt, preferred_element_type=jnp.float32)
            image[s] = y
            x = vec[s]
            return (sums[0] + _fold(x * x), sums[1] + _fold(x * y), sums[2] + _fold(y * y))

        sx, sxy, sy = lax.fori_loop(0, sectors, apply, (zero, zero, zero))
        self_dot, cross_dot, image_dot = _sum_all(sx), _sum_all(sxy), _sum_all(sy)
        rayleigh_now = cross_dot / self_dot
        step_size = 0.5 * jnp.sqrt(self_dot / (image_dot + epsilon))

        def step(s, su):
            x = vec[s]
            u = x - step_size * (image[s] - rayleigh_now * x)
            vec[s] = u
            return su + _fold(u * u)

        su = _sum_all(lax.fori_loop(0, sectors, step, zero))
        scale = lax.rsqrt(su / entries + epsilon)

        def norm(s, carry):
            vec[s] = vec[s] * scale
            return carry

        lax.fori_loop(0, sectors, norm, 0)
        cosine = cross_dot * lax.rsqrt(self_dot * (image_dot + epsilon))
    local = out_ref.shape[0]
    out_ref[...] = vec[pl.ds(place_ref[0] * local, local)]
    cos_ref[...] = jnp.broadcast_to(cosine, cos_ref.shape)


def iterate(table, place, psi, left_env, right_env, local):
    sectors, side, _ = psi.shape
    smem = pl.BlockSpec(memory_space=pltpu.SMEM)
    vmem = pl.BlockSpec(memory_space=pltpu.VMEM)
    envs = left_env.shape[0]
    flops = ITERS * sectors * (2 * envs * (2 * HALO + 1) + 4 * envs) * 2 * side**3
    return pl.pallas_call(
        iterate_kernel,
        out_shape=(
            jax.ShapeDtypeStruct((local, side, side), jnp.float32),
            jax.ShapeDtypeStruct((8, 128), jnp.float32),
        ),
        in_specs=[smem, smem, vmem, vmem, vmem],
        out_specs=(vmem, vmem),
        scratch_shapes=[
            pltpu.VMEM((sectors, side, side), jnp.float32),
            pltpu.VMEM((sectors, side, side), jnp.float32),
            pltpu.VMEM((sectors + 2 * HALO, side, side), jnp.bfloat16),
        ],
        compiler_params=pltpu.CompilerParams(vmem_limit_bytes=48 * 1024 * 1024),
        cost_estimate=pl.CostEstimate(
            flops=flops, transcendentals=0, bytes_accessed=psi.size * 2 + 4 * left_env.size
        ),
    )(table, place, psi, left_env, right_env)


def body(
    psi_start,
    left_terms,
    left_rate,
    right_terms,
    right_rate,
    term_left,
    term_right,
    term_shift,
    term_coef,
):
    with jax.named_scope("psi_gather"):
        psi = lax.all_gather(psi_start[0], "sector", axis=0, tiled=True)
    with jax.named_scope("env_chain"):
        left_env, right_env = chain_envs(left_terms[0], left_rate[0], right_terms[0], right_rate[0])
    with jax.named_scope("env_gather"):
        left_env, right_env = lax.all_gather((left_env, right_env), "sector", axis=1, tiled=True)

    envs = left_env.shape[0]
    with jax.named_scope("term_table"):
        pick_right = (term_right[:, None] == jnp.arange(envs)[None]).astype(jnp.float32)
        pick_left = (term_left[:, None] == jnp.arange(envs)[None]).astype(jnp.float32)
        pick_shift = (term_shift[:, None] == jnp.arange(-HALO, HALO + 1)[None]).astype(jnp.float32)
        table = jnp.sum(
            term_coef[:, None, None, None]
            * pick_right[:, :, None, None]
            * pick_left[:, None, :, None]
            * pick_shift[:, None, None, :],
            axis=0,
        ).reshape(-1)
    local = psi_start.shape[1]
    place = jnp.reshape(lax.axis_index("sector"), (1,)).astype(jnp.int32)
    with jax.named_scope("iterations"):
        mine, cos = iterate(table, place, psi, left_env, right_env, local)
    return (mine[None], jnp.reshape(cos[0, 0], (1,)))


def solution(mesh):
    placed = (
        P("chain", "sector", None, None),
        P("chain", None, "sector", None, None),
        P("chain", None, "sector", None),
        P("chain", None, "sector", None, None),
        P("chain", None, "sector", None),
        P(),
        P(),
        P(),
        P(),
    )
    return jax.shard_map(
        body,
        mesh=mesh,
        in_specs=placed,
        out_specs=(P("chain", "sector", None, None), P("chain")),
        check_vma=False,
    )
```

```python
import functools

import jax
import jax.numpy as jnp
from jax import lax
from jax.experimental import pallas as pl
from jax.experimental.pallas import tpu as pltpu
from jax.sharding import PartitionSpec as P

ITERS = 4
HALO = 2

epsilon = 1e-06


def chain_envs(left_terms, left_rate, right_terms, right_rate):
    count = lax.axis_size("chain")
    shape = left_terms.shape
    width = shape[-1]
    block = left_terms.size // width // count
    rates = jnp.stack([left_rate.reshape(count, block), right_rate.reshape(count, block)], axis=1)
    pieces = []
    rest = rates
    for _ in range(3):
        piece = rest.astype(jnp.bfloat16)
        rest = rest - piece.astype(jnp.float32)
        pieces.append(piece)
    coded = jnp.stack(pieces, axis=1).reshape(count, 6 * block)
    coded = jnp.pad(coded, ((0, 0), (0, 2 * block * width - 6 * block)))
    coded = coded.reshape(count, 2 * block, width)
    packed = jnp.concatenate(
        [left_terms.reshape(count, block, width), right_terms.reshape(count, block, width), coded],
        axis=1,
    )
    spread = lax.all_to_all(packed, "chain", 0, 0, tiled=True)
    got = spread[:, 2 * block :].reshape(count, 2 * block * width)[:, : 6 * block]
    got = got.astype(jnp.float32).reshape(count, 3, 2, block)
    speed = (got[:, 0] + got[:, 1]) + got[:, 2]
    spread = spread[:, : 2 * block].astype(jnp.float32)
    ahead = jnp.cumsum(speed[:, 0], axis=0)
    behind = jnp.cumsum(speed[::-1, 1], axis=0)[::-1]
    order = jnp.arange(count)
    later = (order[:, None] >= order[None, :])[:, :, None]
    earlier = (order[:, None] <= order[None, :])[:, :, None]
    forward = jnp.where(later, ahead[:, None, :] - ahead[None, :, :], 0.0)
    backward = jnp.where(earlier, behind[:, None, :] - behind[None, :, :], 0.0)
    weight = jnp.concatenate(
        [jnp.where(later, jnp.exp(-forward), 0.0), jnp.where(earlier, jnp.exp(-backward), 0.0)],
        axis=2,
    )
    env = jnp.einsum(
        "ghp,hpc->gpc",
        weight,
        spread,
        precision=lax.Precision.HIGHEST,
        preferred_element_type=jnp.float32,
    )
    back = lax.all_to_all(env.astype(jnp.bfloat16), "chain", 0, 0, tiled=True)
    return back[:, :block].reshape(shape), back[:, block:].reshape(shape)


def _sum_all(a):
    return jnp.sum(jnp.sum(a, axis=0, keepdims=True), axis=1, keepdims=True)


def _fold(a):
    return jnp.sum(a.reshape(a.shape[0] // 8, 8, a.shape[1]), axis=0)


def iterate_kernel(table_ref, place_ref, stack_ref, out_ref, cos_ref, vec, image, padded):
    _, sectors, side, _ = stack_ref.shape
    envs = (stack_ref.shape[0] - 1) // 2
    shifts = 2 * HALO + 1
    entries = float(sectors * side * side)
    vec[...] = stack_ref[2 * envs].astype(jnp.float32)
    rim = jnp.zeros((HALO, side, side), jnp.bfloat16)
    padded[0:HALO] = rim
    padded[HALO + sectors : 2 * HALO + sectors] = rim
    nt = (((1,), (1,)), ((), ()))
    zero = jnp.zeros((8, side), jnp.float32)
    cosine = jnp.zeros((1, 1), jnp.float32)
    for iteration in range(ITERS):
        padded[HALO : HALO + sectors] = vec[...].astype(jnp.bfloat16)

        def apply(s, sums):
            lefts = stack_ref[0:envs, s].reshape(envs * side, side)
            parts = [jnp.zeros((side, side), jnp.float32) for _ in range(envs)]
            for t in range(shifts):
                prod = jnp.dot(lefts, padded[s + t], preferred_element_type=jnp.float32)
                prod = prod.astype(jnp.bfloat16).astype(jnp.float32)
                for e in range(envs):
                    piece = prod[e * side : (e + 1) * side]
                    for r in range(envs):
                        coef = table_ref[(r * envs + e) * shifts + t]
                        parts[r] = parts[r] + coef * piece
            y = jnp.zeros((side, side), jnp.float32)
            for r in range(envs):
                high = parts[r].astype(jnp.bfloat16)
                low = (parts[r] - high.astype(jnp.float32)).astype(jnp.bfloat16)
                rt = stack_ref[envs + r, s]
                y = y + lax.dot_general(high, rt, nt, preferred_element_type=jnp.float32)
                y = y + lax.dot_general(low, rt, nt, preferred_element_type=jnp.float32)
            image[s] = y
            x = vec[s]
            return (sums[0] + _fold(x * x), sums[1] + _fold(x * y), sums[2] + _fold(y * y))

        sx, sxy, sy = lax.fori_loop(0, sectors, apply, (zero, zero, zero))
        self_dot, cross_dot, image_dot = _sum_all(sx), _sum_all(sxy), _sum_all(sy)
        rayleigh_now = cross_dot / self_dot
        step_size = 0.5 * jnp.sqrt(self_dot / (image_dot + epsilon))

        def step(s, su):
            x = vec[s]
            u = x - step_size * (image[s] - rayleigh_now * x)
            vec[s] = u
            return su + _fold(u * u)

        su = _sum_all(lax.fori_loop(0, sectors, step, zero))
        scale = lax.rsqrt(su / entries + epsilon)

        def norm(s, carry):
            vec[s] = vec[s] * scale
            return carry

        lax.fori_loop(0, sectors, norm, 0)
        cosine = cross_dot * lax.rsqrt(self_dot * (image_dot + epsilon))
    local = out_ref.shape[0]
    out_ref[...] = vec[pl.ds(place_ref[0] * local, local)]
    cos_ref[...] = jnp.broadcast_to(cosine, cos_ref.shape)


def iterate(table, place, stack, local):
    _, sectors, side, _ = stack.shape
    smem = pl.BlockSpec(memory_space=pltpu.SMEM)
    vmem = pl.BlockSpec(memory_space=pltpu.VMEM)
    envs = (stack.shape[0] - 1) // 2
    flops = ITERS * sectors * (2 * envs * (2 * HALO + 1) + 4 * envs) * 2 * side**3
    return pl.pallas_call(
        iterate_kernel,
        out_shape=(
            jax.ShapeDtypeStruct((local, side, side), jnp.float32),
            jax.ShapeDtypeStruct((8, 128), jnp.float32),
        ),
        in_specs=[smem, smem, vmem],
        out_specs=(vmem, vmem),
        scratch_shapes=[
            pltpu.VMEM((sectors, side, side), jnp.float32),
            pltpu.VMEM((sectors, side, side), jnp.float32),
            pltpu.VMEM((sectors + 2 * HALO, side, side), jnp.bfloat16),
        ],
        compiler_params=pltpu.CompilerParams(vmem_limit_bytes=48 * 1024 * 1024),
        cost_estimate=pl.CostEstimate(
            flops=flops, transcendentals=0, bytes_accessed=stack.size * 2 + 4 * local * side * side
        ),
    )(table, place, stack)


def body(
    psi_start,
    left_terms,
    left_rate,
    right_terms,
    right_rate,
    term_left,
    term_right,
    term_shift,
    term_coef,
):
    with jax.named_scope("env_chain"):
        left_env, right_env = chain_envs(left_terms[0], left_rate[0], right_terms[0], right_rate[0])
    with jax.named_scope("env_gather"):
        stack = lax.all_gather(
            jnp.concatenate([left_env, right_env, psi_start], axis=0), "sector", axis=1, tiled=True
        )

    envs = left_terms.shape[1]
    with jax.named_scope("term_table"):
        pick_right = (term_right[:, None] == jnp.arange(envs)[None]).astype(jnp.float32)
        pick_left = (term_left[:, None] == jnp.arange(envs)[None]).astype(jnp.float32)
        pick_shift = (term_shift[:, None] == jnp.arange(-HALO, HALO + 1)[None]).astype(jnp.float32)
        table = jnp.sum(
            term_coef[:, None, None, None]
            * pick_right[:, :, None, None]
            * pick_left[:, None, :, None]
            * pick_shift[:, None, None, :],
            axis=0,
        ).reshape(-1)
    local = psi_start.shape[1]
    place = jnp.reshape(lax.axis_index("sector"), (1,)).astype(jnp.int32)
    with jax.named_scope("iterations"):
        mine, cos = iterate(table, place, stack, local)
    return (mine[None], jnp.reshape(cos[0, 0], (1,)))


def solution(mesh):
    placed = (
        P("chain", "sector", None, None),
        P("chain", None, "sector", None, None),
        P("chain", None, "sector", None),
        P("chain", None, "sector", None, None),
        P("chain", None, "sector", None),
        P(),
        P(),
        P(),
        P(),
    )
    return jax.shard_map(
        body,
        mesh=mesh,
        in_specs=placed,
        out_specs=(P("chain", "sector", None, None), P("chain")),
        check_vma=False,
    )
```

```python
import functools

import jax
import jax.numpy as jnp
from jax import lax
from jax.experimental import pallas as pl
from jax.experimental.pallas import tpu as pltpu
from jax.sharding import PartitionSpec as P

ITERS = 4
HALO = 2

epsilon = 1e-06


def chain_envs(left_terms, left_rate, right_terms, right_rate):
    count = lax.axis_size("chain")
    shape = left_terms.shape
    width = shape[-1]
    block = left_terms.size // width // count
    rates = jnp.stack([left_rate.reshape(count, block), right_rate.reshape(count, block)], axis=1)
    pieces = []
    rest = rates
    for _ in range(3):
        piece = lax.reduce_precision(rest, exponent_bits=8, mantissa_bits=7)
        rest = rest - piece
        pieces.append(piece.astype(jnp.bfloat16))
    coded = jnp.stack(pieces, axis=1).reshape(count, 6 * block)
    coded = jnp.pad(coded, ((0, 0), (0, 2 * block * width - 6 * block)))
    coded = coded.reshape(count, 2 * block, width)
    packed = jnp.concatenate(
        [left_terms.reshape(count, block, width), right_terms.reshape(count, block, width), coded],
        axis=1,
    )
    spread = lax.all_to_all(packed, "chain", 0, 0, tiled=True)
    got = spread[:, 2 * block :].reshape(count, 2 * block * width)[:, : 6 * block]
    got = got.astype(jnp.float32).reshape(count, 3, 2, block)
    speed = (got[:, 0] + got[:, 1]) + got[:, 2]
    spread = spread[:, : 2 * block].astype(jnp.float32)
    ahead = jnp.cumsum(speed[:, 0], axis=0)
    behind = jnp.cumsum(speed[::-1, 1], axis=0)[::-1]
    order = jnp.arange(count)
    later = (order[:, None] >= order[None, :])[:, :, None]
    earlier = (order[:, None] <= order[None, :])[:, :, None]
    forward = jnp.where(later, ahead[:, None, :] - ahead[None, :, :], 0.0)
    backward = jnp.where(earlier, behind[:, None, :] - behind[None, :, :], 0.0)
    weight = jnp.concatenate(
        [jnp.where(later, jnp.exp(-forward), 0.0), jnp.where(earlier, jnp.exp(-backward), 0.0)],
        axis=2,
    )
    env = jnp.einsum(
        "ghp,hpc->gpc",
        weight,
        spread,
        precision=lax.Precision.HIGHEST,
        preferred_element_type=jnp.float32,
    )
    back = lax.all_to_all(env.astype(jnp.bfloat16), "chain", 0, 0, tiled=True)
    return back[:, :block].reshape(shape), back[:, block:].reshape(shape)


def _sum_all(a):
    return jnp.sum(jnp.sum(a, axis=0, keepdims=True), axis=1, keepdims=True)


def _fold(a):
    return jnp.sum(a.reshape(a.shape[0] // 8, 8, a.shape[1]), axis=0)


def iterate_kernel(table_ref, place_ref, stack_ref, out_ref, cos_ref, vec, image, diag):
    _, sectors, side, _ = stack_ref.shape
    envs = (stack_ref.shape[0] - 1) // 2
    shifts = 2 * HALO + 1
    entries = float(sectors * side * side)
    vec[...] = stack_ref[2 * envs].astype(jnp.float32)
    diag[...] = jnp.zeros(diag.shape, jnp.bfloat16)
    zero = jnp.zeros((8, side), jnp.float32)
    cosine = jnp.zeros((1, 1), jnp.float32)
    for iteration in range(ITERS):

        def fill(s, carry):
            w = vec[s].astype(jnp.bfloat16)
            for e in range(envs):
                diag[s + HALO, e * side : (e + 1) * side, e * side : (e + 1) * side] = w
            return carry

        lax.fori_loop(0, sectors, fill, 0)

        def apply(s, sums):
            lefts = jnp.concatenate([stack_ref[e, s] for e in range(envs)], axis=1)
            parts = [jnp.zeros((side, side), jnp.float32) for _ in range(envs)]
            for t in range(shifts):
                prod = jnp.dot(lefts, diag[s + t], preferred_element_type=jnp.float32)
                prod = prod.astype(jnp.bfloat16).astype(jnp.float32)
                for e in range(envs):
                    piece = prod[:, e * side : (e + 1) * side]
                    for r in range(envs):
                        coef = table_ref[(r * envs + e) * shifts + t]
                        parts[r] = parts[r] + coef * piece
            halves = []
            rights = []
            for r in range(envs):
                high = parts[r].astype(jnp.bfloat16)
                low = (parts[r] - high.astype(jnp.float32)).astype(jnp.bfloat16)
                halves += [high, low]
                rt = stack_ref[envs + r, s]
                rights += [rt, rt]
            y = jnp.dot(
                jnp.concatenate(halves, axis=1),
                jnp.concatenate(rights, axis=0),
                preferred_element_type=jnp.float32,
            )
            image[s] = y
            x = vec[s]
            return (sums[0] + _fold(x * x), sums[1] + _fold(x * y), sums[2] + _fold(y * y))

        sx, sxy, sy = lax.fori_loop(0, sectors, apply, (zero, zero, zero))
        self_dot, cross_dot, image_dot = _sum_all(sx), _sum_all(sxy), _sum_all(sy)
        rayleigh_now = cross_dot / self_dot
        step_size = 0.5 * jnp.sqrt(self_dot / (image_dot + epsilon))

        def step(s, su):
            x = vec[s]
            u = x - step_size * (image[s] - rayleigh_now * x)
            vec[s] = u
            return su + _fold(u * u)

        su = _sum_all(lax.fori_loop(0, sectors, step, zero))
        scale = lax.rsqrt(su / entries + epsilon)

        def norm(s, carry):
            vec[s] = vec[s] * scale
            return carry

        lax.fori_loop(0, sectors, norm, 0)
        cosine = cross_dot * lax.rsqrt(self_dot * (image_dot + epsilon))
    local = out_ref.shape[0]
    out_ref[...] = vec[pl.ds(place_ref[0] * local, local)]
    cos_ref[...] = jnp.broadcast_to(cosine, cos_ref.shape)


def iterate(table, place, stack, local):
    _, sectors, side, _ = stack.shape
    smem = pl.BlockSpec(memory_space=pltpu.SMEM)
    vmem = pl.BlockSpec(memory_space=pltpu.VMEM)
    envs = (stack.shape[0] - 1) // 2
    flops = ITERS * sectors * (2 * envs * (2 * HALO + 1) + 4 * envs) * 2 * side**3
    return pl.pallas_call(
        iterate_kernel,
        out_shape=(
            jax.ShapeDtypeStruct((local, side, side), jnp.float32),
            jax.ShapeDtypeStruct((8, 128), jnp.float32),
        ),
        in_specs=[smem, smem, vmem],
        out_specs=(vmem, vmem),
        scratch_shapes=[
            pltpu.VMEM((sectors, side, side), jnp.float32),
            pltpu.VMEM((sectors, side, side), jnp.float32),
            pltpu.VMEM((sectors + 2 * HALO, envs * side, envs * side), jnp.bfloat16),
        ],
        compiler_params=pltpu.CompilerParams(vmem_limit_bytes=48 * 1024 * 1024),
        cost_estimate=pl.CostEstimate(
            flops=flops, transcendentals=0, bytes_accessed=stack.size * 2 + 4 * local * side * side
        ),
    )(table, place, stack)


def body(
    psi_start,
    left_terms,
    left_rate,
    right_terms,
    right_rate,
    term_left,
    term_right,
    term_shift,
    term_coef,
):
    with jax.named_scope("env_chain"):
        left_env, right_env = chain_envs(left_terms[0], left_rate[0], right_terms[0], right_rate[0])
    with jax.named_scope("env_gather"):
        stack = lax.all_gather(
            jnp.concatenate([left_env, jnp.swapaxes(right_env, -1, -2), psi_start], axis=0),
            "sector",
            axis=1,
            tiled=True,
        )

    envs = left_terms.shape[1]
    with jax.named_scope("term_table"):
        pick_right = (term_right[:, None] == jnp.arange(envs)[None]).astype(jnp.float32)
        pick_left = (term_left[:, None] == jnp.arange(envs)[None]).astype(jnp.float32)
        pick_shift = (term_shift[:, None] == jnp.arange(-HALO, HALO + 1)[None]).astype(jnp.float32)
        table = jnp.sum(
            term_coef[:, None, None, None]
            * pick_right[:, :, None, None]
            * pick_left[:, None, :, None]
            * pick_shift[:, None, None, :],
            axis=0,
        ).reshape(-1)
    local = psi_start.shape[1]
    place = jnp.reshape(lax.axis_index("sector"), (1,)).astype(jnp.int32)
    with jax.named_scope("iterations"):
        mine, cos = iterate(table, place, stack, local)
    return (mine[None], jnp.reshape(cos[0, 0], (1,)))


def solution(mesh):
    placed = (
        P("chain", "sector", None, None),
        P("chain", None, "sector", None, None),
        P("chain", None, "sector", None),
        P("chain", None, "sector", None, None),
        P("chain", None, "sector", None),
        P(),
        P(),
        P(),
        P(),
    )
    return jax.shard_map(
        body,
        mesh=mesh,
        in_specs=placed,
        out_specs=(P("chain", "sector", None, None), P("chain")),
        check_vma=False,
    )
```

```python
import functools

import jax
import jax.numpy as jnp
from jax import lax
from jax.experimental import pallas as pl
from jax.experimental.pallas import tpu as pltpu
from jax.sharding import PartitionSpec as P

ITERS = 4
HALO = 2

epsilon = 1e-06


def chain_envs(left_terms, left_rate, right_terms, right_rate):
    count = lax.axis_size("chain")
    shape = left_terms.shape
    width = shape[-1]
    block = left_terms.size // width // count
    packed = jnp.concatenate(
        [left_terms.reshape(count, block, width), right_terms.reshape(count, block, width)], axis=1
    )
    spread = lax.all_to_all(packed, "chain", 0, 0, tiled=True).astype(jnp.float32)
    rates = jnp.stack([left_rate.reshape(1, count * block), right_rate.reshape(1, count * block)])
    rates = lax.all_gather(rates, "chain", axis=1, tiled=True)
    rates = rates.reshape(2, count, count, block)
    speed = jnp.swapaxes(lax.dynamic_index_in_dim(rates, lax.axis_index("chain"), 2, False), 0, 1)
    ahead = jnp.cumsum(speed[:, 0], axis=0)
    behind = jnp.cumsum(speed[::-1, 1], axis=0)[::-1]
    order = jnp.arange(count)
    later = (order[:, None] >= order[None, :])[:, :, None]
    earlier = (order[:, None] <= order[None, :])[:, :, None]
    forward = jnp.where(later, ahead[:, None, :] - ahead[None, :, :], 0.0)
    backward = jnp.where(earlier, behind[:, None, :] - behind[None, :, :], 0.0)
    weight = jnp.concatenate(
        [jnp.where(later, jnp.exp(-forward), 0.0), jnp.where(earlier, jnp.exp(-backward), 0.0)],
        axis=2,
    )
    env = jnp.einsum(
        "ghp,hpc->gpc",
        weight,
        spread,
        precision=lax.Precision.HIGHEST,
        preferred_element_type=jnp.float32,
    )
    back = lax.all_to_all(env.astype(jnp.bfloat16), "chain", 0, 0, tiled=True)
    return back[:, :block].reshape(shape), back[:, block:].reshape(shape)


def _sum_all(a):
    return jnp.sum(jnp.sum(a, axis=0, keepdims=True), axis=1, keepdims=True)


def _fold(a):
    return jnp.sum(a.reshape(a.shape[0] // 8, 8, a.shape[1]), axis=0)


def iterate_kernel(table_ref, place_ref, stack_ref, out_ref, cos_ref, vec, image, diag):
    _, sectors, side, _ = stack_ref.shape
    envs = (stack_ref.shape[0] - 1) // 2
    shifts = 2 * HALO + 1
    entries = float(sectors * side * side)
    vec[...] = stack_ref[2 * envs].astype(jnp.float32)
    diag[...] = jnp.zeros(diag.shape, jnp.bfloat16)
    zero = jnp.zeros((8, side), jnp.float32)
    cosine = jnp.zeros((1, 1), jnp.float32)
    scale = None
    for iteration in range(ITERS):

        def fill(s, carry):
            x = vec[s]
            if scale is not None:
                x = x * scale
                vec[s] = x
            w = x.astype(jnp.bfloat16)
            for e in range(envs):
                diag[s + HALO, e * side : (e + 1) * side, e * side : (e + 1) * side] = w
            return carry

        lax.fori_loop(0, sectors, fill, 0)

        def apply(s, sums):
            lefts = jnp.concatenate([stack_ref[e, s] for e in range(envs)], axis=1)
            parts = [jnp.zeros((side, side), jnp.float32) for _ in range(envs)]
            for t in range(shifts):
                prod = jnp.dot(lefts, diag[s + t], preferred_element_type=jnp.float32)
                prod = prod.astype(jnp.bfloat16).astype(jnp.float32)
                for e in range(envs):
                    piece = prod[:, e * side : (e + 1) * side]
                    for r in range(envs):
                        coef = table_ref[(r * envs + e) * shifts + t]
                        parts[r] = parts[r] + coef * piece
            halves = []
            rights = []
            for r in range(envs):
                high = parts[r].astype(jnp.bfloat16)
                low = (parts[r] - high.astype(jnp.float32)).astype(jnp.bfloat16)
                halves += [high, low]
                rt = stack_ref[envs + r, s]
                rights += [rt, rt]
            y = jnp.dot(
                jnp.concatenate(halves, axis=1),
                jnp.concatenate(rights, axis=0),
                preferred_element_type=jnp.float32,
            )
            image[s] = y
            x = vec[s]
            return (sums[0] + _fold(x * x), sums[1] + _fold(x * y), sums[2] + _fold(y * y))

        sx, sxy, sy = lax.fori_loop(0, sectors, apply, (zero, zero, zero))
        self_dot, cross_dot, image_dot = _sum_all(sx), _sum_all(sxy), _sum_all(sy)
        rayleigh_now = cross_dot / self_dot
        step_size = 0.5 * jnp.sqrt(self_dot / (image_dot + epsilon))

        def step(s, su):
            x = vec[s]
            u = x - step_size * (image[s] - rayleigh_now * x)
            vec[s] = u
            return su + _fold(u * u)

        su = _sum_all(lax.fori_loop(0, sectors, step, zero))
        scale = lax.rsqrt(su / entries + epsilon)
        cosine = cross_dot * lax.rsqrt(self_dot * (image_dot + epsilon))
    local = out_ref.shape[0]
    out_ref[...] = vec[pl.ds(place_ref[0] * local, local)] * scale
    cos_ref[...] = jnp.broadcast_to(cosine, cos_ref.shape)


def iterate(table, place, stack, local):
    _, sectors, side, _ = stack.shape
    smem = pl.BlockSpec(memory_space=pltpu.SMEM)
    vmem = pl.BlockSpec(memory_space=pltpu.VMEM)
    envs = (stack.shape[0] - 1) // 2
    flops = ITERS * sectors * (2 * envs * (2 * HALO + 1) + 4 * envs) * 2 * side**3
    return pl.pallas_call(
        iterate_kernel,
        out_shape=(
            jax.ShapeDtypeStruct((local, side, side), jnp.float32),
            jax.ShapeDtypeStruct((8, 128), jnp.float32),
        ),
        in_specs=[smem, smem, vmem],
        out_specs=(vmem, vmem),
        scratch_shapes=[
            pltpu.VMEM((sectors, side, side), jnp.float32),
            pltpu.VMEM((sectors, side, side), jnp.float32),
            pltpu.VMEM((sectors + 2 * HALO, envs * side, envs * side), jnp.bfloat16),
        ],
        compiler_params=pltpu.CompilerParams(vmem_limit_bytes=48 * 1024 * 1024),
        cost_estimate=pl.CostEstimate(
            flops=flops, transcendentals=0, bytes_accessed=stack.size * 2 + 4 * local * side * side
        ),
    )(table, place, stack)


def body(
    psi_start,
    left_terms,
    left_rate,
    right_terms,
    right_rate,
    term_left,
    term_right,
    term_shift,
    term_coef,
):
    with jax.named_scope("env_chain"):
        left_env, right_env = chain_envs(left_terms[0], left_rate[0], right_terms[0], right_rate[0])
    with jax.named_scope("env_gather"):
        stack = lax.all_gather(
            jnp.concatenate([left_env, jnp.swapaxes(right_env, -1, -2), psi_start], axis=0),
            "sector",
            axis=1,
            tiled=True,
        )

    envs = left_terms.shape[1]
    with jax.named_scope("term_table"):
        pick_right = (term_right[:, None] == jnp.arange(envs)[None]).astype(jnp.float32)
        pick_left = (term_left[:, None] == jnp.arange(envs)[None]).astype(jnp.float32)
        pick_shift = (term_shift[:, None] == jnp.arange(-HALO, HALO + 1)[None]).astype(jnp.float32)
        table = jnp.sum(
            term_coef[:, None, None, None]
            * pick_right[:, :, None, None]
            * pick_left[:, None, :, None]
            * pick_shift[:, None, None, :],
            axis=0,
        ).reshape(-1)
    local = psi_start.shape[1]
    place = jnp.reshape(lax.axis_index("sector"), (1,)).astype(jnp.int32)
    with jax.named_scope("iterations"):
        mine, cos = iterate(table, place, stack, local)
    return (mine[None], jnp.reshape(cos[0, 0], (1,)))


def solution(mesh):
    placed = (
        P("chain", "sector", None, None),
        P("chain", None, "sector", None, None),
        P("chain", None, "sector", None),
        P("chain", None, "sector", None, None),
        P("chain", None, "sector", None),
        P(),
        P(),
        P(),
        P(),
    )
    return jax.shard_map(
        body,
        mesh=mesh,
        in_specs=placed,
        out_specs=(P("chain", "sector", None, None), P("chain")),
        check_vma=False,
    )
```

```python
import functools

import jax
import jax.numpy as jnp
from jax import lax
from jax.experimental import pallas as pl
from jax.experimental.pallas import tpu as pltpu
from jax.sharding import PartitionSpec as P

ITERS = 4
HALO = 2

epsilon = 1e-06


def chain_envs(left_terms, left_rate, right_terms, right_rate):
    count = lax.axis_size("chain")
    shape = left_terms.shape
    width = shape[-1]
    block = left_terms.size // width // count
    rates = jnp.stack([left_rate.reshape(count, block), right_rate.reshape(count, block)], axis=1)
    pieces = []
    rest = rates
    for _ in range(3):
        piece = lax.reduce_precision(rest, exponent_bits=8, mantissa_bits=7)
        rest = rest - piece
        pieces.append(piece.astype(jnp.bfloat16))
    coded = jnp.stack(pieces, axis=1).reshape(count, 6 * block)
    coded = jnp.pad(coded, ((0, 0), (0, 2 * block * width - 6 * block)))
    coded = coded.reshape(count, 2 * block, width)
    packed = jnp.concatenate(
        [left_terms.reshape(count, block, width), right_terms.reshape(count, block, width), coded],
        axis=1,
    )
    spread = lax.all_to_all(packed, "chain", 0, 0, tiled=True)
    got = spread[:, 2 * block :].reshape(count, 2 * block * width)[:, : 6 * block]
    got = got.astype(jnp.float32).reshape(count, 3, 2, block)
    speed = (got[:, 0] + got[:, 1]) + got[:, 2]
    spread = spread[:, : 2 * block].astype(jnp.float32)
    ahead = jnp.cumsum(speed[:, 0], axis=0)
    behind = jnp.cumsum(speed[::-1, 1], axis=0)[::-1]
    order = jnp.arange(count)
    later = (order[:, None] >= order[None, :])[:, :, None]
    earlier = (order[:, None] <= order[None, :])[:, :, None]
    forward = jnp.where(later, ahead[:, None, :] - ahead[None, :, :], 0.0)
    backward = jnp.where(earlier, behind[:, None, :] - behind[None, :, :], 0.0)
    weight = jnp.concatenate(
        [jnp.where(later, jnp.exp(-forward), 0.0), jnp.where(earlier, jnp.exp(-backward), 0.0)],
        axis=2,
    )
    env = jnp.einsum(
        "ghp,hpc->gpc",
        weight,
        spread,
        precision=lax.Precision.HIGHEST,
        preferred_element_type=jnp.float32,
    )
    back = lax.all_to_all(env.astype(jnp.bfloat16), "chain", 0, 0, tiled=True)
    return back[:, :block].reshape(shape), back[:, block:].reshape(shape)


def _sum_all(a):
    return jnp.sum(jnp.sum(a, axis=0, keepdims=True), axis=1, keepdims=True)


def _fold(a):
    return jnp.sum(a.reshape(a.shape[0] // 8, 8, a.shape[1]), axis=0)


def iterate_kernel(table_ref, place_ref, stack_ref, out_ref, cos_ref, vec, image, diag):
    _, sectors, side, _ = stack_ref.shape
    envs = (stack_ref.shape[0] - 1) // 2
    shifts = 2 * HALO + 1
    entries = float(sectors * side * side)
    vec[...] = stack_ref[2 * envs].astype(jnp.float32)
    diag[...] = jnp.zeros(diag.shape, jnp.bfloat16)
    zero = jnp.zeros((8, side), jnp.float32)
    cosine = jnp.zeros((1, 1), jnp.float32)

    def fill(s, carry):
        w = vec[s].astype(jnp.bfloat16)
        for e in range(envs):
            diag[s + HALO, e * side : (e + 1) * side, e * side : (e + 1) * side] = w
        return carry

    lax.fori_loop(0, sectors, fill, 0)
    for iteration in range(ITERS):

        def apply(s, sums):
            lefts = jnp.concatenate([stack_ref[e, s] for e in range(envs)], axis=1)
            parts = [jnp.zeros((side, side), jnp.float32) for _ in range(envs)]
            for t in range(shifts):
                prod = jnp.dot(lefts, diag[s + t], preferred_element_type=jnp.float32)
                prod = prod.astype(jnp.bfloat16).astype(jnp.float32)
                for e in range(envs):
                    piece = prod[:, e * side : (e + 1) * side]
                    for r in range(envs):
                        coef = table_ref[(r * envs + e) * shifts + t]
                        parts[r] = parts[r] + coef * piece
            halves = []
            rights = []
            for r in range(envs):
                high = parts[r].astype(jnp.bfloat16)
                low = (parts[r] - high.astype(jnp.float32)).astype(jnp.bfloat16)
                halves += [high, low]
                rt = stack_ref[envs + r, s]
                rights += [rt, rt]
            y = jnp.dot(
                jnp.concatenate(halves, axis=1),
                jnp.concatenate(rights, axis=0),
                preferred_element_type=jnp.float32,
            )
            image[s] = y
            x = vec[s]
            return (sums[0] + _fold(x * x), sums[1] + _fold(x * y), sums[2] + _fold(y * y))

        sx, sxy, sy = lax.fori_loop(0, sectors, apply, (zero, zero, zero))
        self_dot, cross_dot, image_dot = _sum_all(sx), _sum_all(sxy), _sum_all(sy)
        rayleigh_now = cross_dot / self_dot
        step_size = 0.5 * jnp.sqrt(self_dot / (image_dot + epsilon))

        keep = 1.0 + step_size * rayleigh_now
        update_sq = (
            keep * keep * self_dot
            - 2.0 * keep * step_size * cross_dot
            + step_size * step_size * image_dot
        )
        scale = lax.rsqrt(update_sq / entries + epsilon)

        def step(s, carry):
            x = vec[s]
            u = x - step_size * (image[s] - rayleigh_now * x)
            x = u * scale
            vec[s] = x
            if iteration + 1 < ITERS:
                w = x.astype(jnp.bfloat16)
                for e in range(envs):
                    diag[s + HALO, e * side : (e + 1) * side, e * side : (e + 1) * side] = w
            return carry

        lax.fori_loop(0, sectors, step, 0)
        cosine = cross_dot * lax.rsqrt(self_dot * (image_dot + epsilon))
    local = out_ref.shape[0]
    out_ref[...] = vec[pl.ds(place_ref[0] * local, local)]
    cos_ref[...] = jnp.broadcast_to(cosine, cos_ref.shape)


def iterate(table, place, stack, local):
    _, sectors, side, _ = stack.shape
    smem = pl.BlockSpec(memory_space=pltpu.SMEM)
    vmem = pl.BlockSpec(memory_space=pltpu.VMEM)
    envs = (stack.shape[0] - 1) // 2
    flops = ITERS * sectors * (2 * envs * (2 * HALO + 1) + 4 * envs) * 2 * side**3
    return pl.pallas_call(
        iterate_kernel,
        out_shape=(
            jax.ShapeDtypeStruct((local, side, side), jnp.float32),
            jax.ShapeDtypeStruct((8, 128), jnp.float32),
        ),
        in_specs=[smem, smem, vmem],
        out_specs=(vmem, vmem),
        scratch_shapes=[
            pltpu.VMEM((sectors, side, side), jnp.float32),
            pltpu.VMEM((sectors, side, side), jnp.float32),
            pltpu.VMEM((sectors + 2 * HALO, envs * side, envs * side), jnp.bfloat16),
        ],
        compiler_params=pltpu.CompilerParams(vmem_limit_bytes=48 * 1024 * 1024),
        cost_estimate=pl.CostEstimate(
            flops=flops,
            transcendentals=0,
            bytes_accessed=stack.size * 2 + 4 * local * side * side,
        ),
    )(table, place, stack)


def body(
    psi_start,
    left_terms,
    left_rate,
    right_terms,
    right_rate,
    term_left,
    term_right,
    term_shift,
    term_coef,
):
    with jax.named_scope("env_chain"):
        left_env, right_env = chain_envs(left_terms[0], left_rate[0], right_terms[0], right_rate[0])
    with jax.named_scope("env_gather"):
        stack = lax.all_gather(
            jnp.concatenate([left_env, jnp.swapaxes(right_env, -1, -2), psi_start], axis=0),
            "sector",
            axis=1,
            tiled=True,
        )

    envs = left_terms.shape[1]
    with jax.named_scope("term_table"):
        pick_right = (term_right[:, None] == jnp.arange(envs)[None]).astype(jnp.float32)
        pick_left = (term_left[:, None] == jnp.arange(envs)[None]).astype(jnp.float32)
        pick_shift = (term_shift[:, None] == jnp.arange(-HALO, HALO + 1)[None]).astype(jnp.float32)
        table = jnp.sum(
            term_coef[:, None, None, None]
            * pick_right[:, :, None, None]
            * pick_left[:, None, :, None]
            * pick_shift[:, None, None, :],
            axis=0,
        ).reshape(-1)
    local = psi_start.shape[1]
    place = jnp.reshape(lax.axis_index("sector"), (1,)).astype(jnp.int32)
    with jax.named_scope("iterations"):
        mine, cos = iterate(table, place, stack, local)
    return (mine[None], jnp.reshape(cos[0, 0], (1,)))


def solution(mesh):
    placed = (
        P("chain", "sector", None, None),
        P("chain", None, "sector", None, None),
        P("chain", None, "sector", None),
        P("chain", None, "sector", None, None),
        P("chain", None, "sector", None),
        P(),
        P(),
        P(),
        P(),
    )
    return jax.shard_map(
        body,
        mesh=mesh,
        in_specs=placed,
        out_specs=(P("chain", "sector", None, None), P("chain")),
        check_vma=False,
    )
```

```python
import functools

import jax
import jax.numpy as jnp
from jax import lax
from jax.experimental import pallas as pl
from jax.experimental.pallas import tpu as pltpu
from jax.sharding import PartitionSpec as P

ITERS = 4
HALO = 2

epsilon = 1e-06


def chain_envs(left_terms, left_rate, right_terms, right_rate):
    count = lax.axis_size("chain")
    shape = left_terms.shape
    width = shape[-1]
    block = left_terms.size // width // count
    rates = jnp.stack([left_rate.reshape(count, block), right_rate.reshape(count, block)], axis=1)
    pieces = []
    rest = rates
    for _ in range(3):
        piece = lax.reduce_precision(rest, exponent_bits=8, mantissa_bits=7)
        rest = rest - piece
        pieces.append(piece.astype(jnp.bfloat16))
    coded = jnp.stack(pieces, axis=1).reshape(count, 6 * block)
    coded = jnp.pad(coded, ((0, 0), (0, 2 * block * width - 6 * block)))
    coded = coded.reshape(count, 2 * block, width)
    packed = jnp.concatenate(
        [left_terms.reshape(count, block, width), right_terms.reshape(count, block, width), coded],
        axis=1,
    )
    spread = lax.all_to_all(packed, "chain", 0, 0, tiled=True)
    got = spread[:, 2 * block :].reshape(count, 2 * block * width)[:, : 6 * block]
    got = got.astype(jnp.float32).reshape(count, 3, 2, block)
    speed = (got[:, 0] + got[:, 1]) + got[:, 2]
    spread = spread[:, : 2 * block].astype(jnp.float32)
    ahead = jnp.cumsum(speed[:, 0], axis=0)
    behind = jnp.cumsum(speed[::-1, 1], axis=0)[::-1]
    order = jnp.arange(count)
    later = (order[:, None] >= order[None, :])[:, :, None]
    earlier = (order[:, None] <= order[None, :])[:, :, None]
    forward = jnp.where(later, ahead[:, None, :] - ahead[None, :, :], 0.0)
    backward = jnp.where(earlier, behind[:, None, :] - behind[None, :, :], 0.0)
    weight = jnp.concatenate(
        [jnp.where(later, jnp.exp(-forward), 0.0), jnp.where(earlier, jnp.exp(-backward), 0.0)],
        axis=2,
    )
    env = jnp.einsum(
        "ghp,hpc->gpc",
        weight,
        spread,
        precision=lax.Precision.HIGHEST,
        preferred_element_type=jnp.float32,
    )
    back = lax.all_to_all(env.astype(jnp.bfloat16), "chain", 0, 0, tiled=True)
    return back[:, :block].reshape(shape), back[:, block:].reshape(shape)


def _sum_all(a):
    return jnp.sum(jnp.sum(a, axis=0, keepdims=True), axis=1, keepdims=True)


def _fold(a):
    return jnp.sum(a.reshape(a.shape[0] // 8, 8, a.shape[1]), axis=0)


def iterate_kernel(table_ref, place_ref, stack_ref, out_ref, cos_ref, vec, image, diag):
    _, sectors, side, _ = stack_ref.shape
    envs = (stack_ref.shape[0] - 1) // 2
    shifts = 2 * HALO + 1
    entries = float(sectors * side * side)
    vec[...] = stack_ref[2 * envs].astype(jnp.float32)
    diag[...] = jnp.zeros(diag.shape, jnp.bfloat16)
    zero = jnp.zeros((8, side), jnp.float32)
    cosine = jnp.zeros((1, 1), jnp.float32)

    def fill(s, carry):
        w = vec[s].astype(jnp.bfloat16)
        for e in range(envs):
            diag[s + HALO, e * side : (e + 1) * side, e * side : (e + 1) * side] = w
        return carry

    lax.fori_loop(0, sectors, fill, 0)
    for iteration in range(ITERS):

        def apply(s, sums):
            lefts = jnp.concatenate([stack_ref[e, s] for e in range(envs)], axis=1)
            parts = [jnp.zeros((side, side), jnp.float32) for _ in range(envs)]
            for t in range(shifts):
                prod = jnp.dot(lefts, diag[s + t], preferred_element_type=jnp.float32)
                prod = prod.astype(jnp.bfloat16).astype(jnp.float32)
                for e in range(envs):
                    piece = prod[:, e * side : (e + 1) * side]
                    for r in range(envs):
                        coef = table_ref[(r * envs + e) * shifts + t]
                        parts[r] = parts[r] + coef * piece
            halves = []
            rights = []
            for r in range(envs):
                high = parts[r].astype(jnp.bfloat16)
                low = (parts[r] - high.astype(jnp.float32)).astype(jnp.bfloat16)
                halves += [high, low]
                rt = stack_ref[envs + r, s]
                rights += [rt, rt]
            y = jnp.dot(
                jnp.concatenate(halves, axis=1),
                jnp.concatenate(rights, axis=0),
                preferred_element_type=jnp.float32,
            )
            image[s] = y
            x = vec[s]
            return (sums[0] + _fold(x * x), sums[1] + _fold(x * y), sums[2] + _fold(y * y))

        sx, sxy, sy = lax.fori_loop(0, sectors, apply, (zero, zero, zero), unroll=16)
        self_dot, cross_dot, image_dot = _sum_all(sx), _sum_all(sxy), _sum_all(sy)
        rayleigh_now = cross_dot / self_dot
        step_size = 0.5 * jnp.sqrt(self_dot / (image_dot + epsilon))

        keep = 1.0 + step_size * rayleigh_now
        update_sq = (
            keep * keep * self_dot
            - 2.0 * keep * step_size * cross_dot
            + step_size * step_size * image_dot
        )
        scale = lax.rsqrt(update_sq / entries + epsilon)

        def step(s, carry):
            x = vec[s]
            u = x - step_size * (image[s] - rayleigh_now * x)
            x = u * scale
            vec[s] = x
            if iteration + 1 < ITERS:
                w = x.astype(jnp.bfloat16)
                for e in range(envs):
                    diag[s + HALO, e * side : (e + 1) * side, e * side : (e + 1) * side] = w
            return carry

        lax.fori_loop(0, sectors, step, 0, unroll=4)
        cosine = cross_dot * lax.rsqrt(self_dot * (image_dot + epsilon))
    local = out_ref.shape[0]
    out_ref[...] = vec[pl.ds(place_ref[0] * local, local)]
    cos_ref[...] = jnp.broadcast_to(cosine, cos_ref.shape)


def iterate(table, place, stack, local):
    _, sectors, side, _ = stack.shape
    smem = pl.BlockSpec(memory_space=pltpu.SMEM)
    vmem = pl.BlockSpec(memory_space=pltpu.VMEM)
    envs = (stack.shape[0] - 1) // 2
    flops = ITERS * sectors * (2 * envs * (2 * HALO + 1) + 4 * envs) * 2 * side**3
    return pl.pallas_call(
        iterate_kernel,
        out_shape=(
            jax.ShapeDtypeStruct((local, side, side), jnp.float32),
            jax.ShapeDtypeStruct((8, 128), jnp.float32),
        ),
        in_specs=[smem, smem, vmem],
        out_specs=(vmem, vmem),
        scratch_shapes=[
            pltpu.VMEM((sectors, side, side), jnp.float32),
            pltpu.VMEM((sectors, side, side), jnp.float32),
            pltpu.VMEM((sectors + 2 * HALO, envs * side, envs * side), jnp.bfloat16),
        ],
        compiler_params=pltpu.CompilerParams(vmem_limit_bytes=48 * 1024 * 1024),
        cost_estimate=pl.CostEstimate(
            flops=flops,
            transcendentals=0,
            bytes_accessed=stack.size * 2 + 4 * local * side * side,
        ),
    )(table, place, stack)


def body(
    psi_start,
    left_terms,
    left_rate,
    right_terms,
    right_rate,
    term_left,
    term_right,
    term_shift,
    term_coef,
):
    with jax.named_scope("env_chain"):
        left_env, right_env = chain_envs(left_terms[0], left_rate[0], right_terms[0], right_rate[0])
    with jax.named_scope("env_gather"):
        stack = lax.all_gather(
            jnp.concatenate([left_env, jnp.swapaxes(right_env, -1, -2), psi_start], axis=0),
            "sector",
            axis=1,
            tiled=True,
        )

    envs = left_terms.shape[1]
    with jax.named_scope("term_table"):
        pick_right = (term_right[:, None] == jnp.arange(envs)[None]).astype(jnp.float32)
        pick_left = (term_left[:, None] == jnp.arange(envs)[None]).astype(jnp.float32)
        pick_shift = (term_shift[:, None] == jnp.arange(-HALO, HALO + 1)[None]).astype(jnp.float32)
        table = jnp.sum(
            term_coef[:, None, None, None]
            * pick_right[:, :, None, None]
            * pick_left[:, None, :, None]
            * pick_shift[:, None, None, :],
            axis=0,
        ).reshape(-1)
    local = psi_start.shape[1]
    place = jnp.reshape(lax.axis_index("sector"), (1,)).astype(jnp.int32)
    with jax.named_scope("iterations"):
        mine, cos = iterate(table, place, stack, local)
    return (mine[None], jnp.reshape(cos[0, 0], (1,)))


def solution(mesh):
    placed = (
        P("chain", "sector", None, None),
        P("chain", None, "sector", None, None),
        P("chain", None, "sector", None),
        P("chain", None, "sector", None, None),
        P("chain", None, "sector", None),
        P(),
        P(),
        P(),
        P(),
    )
    return jax.shard_map(
        body,
        mesh=mesh,
        in_specs=placed,
        out_specs=(P("chain", "sector", None, None), P("chain")),
        check_vma=False,
    )
```

```python
import functools

import jax
import jax.numpy as jnp
from jax import lax
from jax.experimental import pallas as pl
from jax.experimental.pallas import tpu as pltpu
from jax.sharding import PartitionSpec as P

ITERS = 4
HALO = 2

epsilon = 1e-06


def chain_envs(left_terms, left_rate, right_terms, right_rate):
    count = lax.axis_size("chain")
    shape = left_terms.shape
    width = shape[-1]
    block = left_terms.size // width // count
    rates = jnp.stack([left_rate.reshape(count, block), right_rate.reshape(count, block)], axis=1)
    pieces = []
    rest = rates
    for _ in range(3):
        piece = lax.reduce_precision(rest, exponent_bits=8, mantissa_bits=7)
        rest = rest - piece
        pieces.append(piece.astype(jnp.bfloat16))
    coded = jnp.stack(pieces, axis=1).reshape(count, 6 * block)
    coded = jnp.pad(coded, ((0, 0), (0, 2 * block * width - 6 * block)))
    coded = coded.reshape(count, 2 * block, width)
    packed = jnp.concatenate(
        [left_terms.reshape(count, block, width), right_terms.reshape(count, block, width), coded],
        axis=1,
    )
    spread = lax.all_to_all(packed, "chain", 0, 0, tiled=True)
    got = spread[:, 2 * block :].reshape(count, 2 * block * width)[:, : 6 * block]
    got = got.astype(jnp.float32).reshape(count, 3, 2, block)
    speed = (got[:, 0] + got[:, 1]) + got[:, 2]
    spread = spread[:, : 2 * block].astype(jnp.float32)
    ahead = jnp.cumsum(speed[:, 0], axis=0)
    behind = jnp.cumsum(speed[::-1, 1], axis=0)[::-1]
    order = jnp.arange(count)
    later = (order[:, None] >= order[None, :])[:, :, None]
    earlier = (order[:, None] <= order[None, :])[:, :, None]
    forward = jnp.where(later, ahead[:, None, :] - ahead[None, :, :], 0.0)
    backward = jnp.where(earlier, behind[:, None, :] - behind[None, :, :], 0.0)
    weight = jnp.concatenate(
        [jnp.where(later, jnp.exp(-forward), 0.0), jnp.where(earlier, jnp.exp(-backward), 0.0)],
        axis=2,
    )
    env = jnp.einsum(
        "ghp,hpc->gpc",
        weight,
        spread,
        precision=lax.Precision.HIGHEST,
        preferred_element_type=jnp.float32,
    )
    back = lax.all_to_all(env.astype(jnp.bfloat16), "chain", 0, 0, tiled=True)
    return back[:, :block].reshape(shape), back[:, block:].reshape(shape)


def _sum_all(a):
    return jnp.sum(jnp.sum(a, axis=0, keepdims=True), axis=1, keepdims=True)


def _fold(a):
    return jnp.sum(a.reshape(a.shape[0] // 8, 8, a.shape[1]), axis=0)


def iterate_kernel(table_ref, place_ref, psi_ref, stack_ref, out_ref, cos_ref, vec, image, diag):
    _, sectors, side, _ = stack_ref.shape
    envs = stack_ref.shape[0] // 2
    shifts = 2 * HALO + 1
    entries = float(sectors * side * side)
    vec[...] = psi_ref[...]
    diag[...] = jnp.zeros(diag.shape, jnp.bfloat16)
    zero = jnp.zeros((8, side), jnp.float32)
    cosine = jnp.zeros((1, 1), jnp.float32)

    def fill(s, carry):
        w = vec[s].astype(jnp.bfloat16)
        for e in range(envs):
            diag[s + HALO, e * side : (e + 1) * side, e * side : (e + 1) * side] = w
        return carry

    lax.fori_loop(0, sectors, fill, 0)
    for iteration in range(ITERS):

        def apply(s, sums):
            lefts = jnp.concatenate([stack_ref[e, s] for e in range(envs)], axis=1)
            parts = [jnp.zeros((side, side), jnp.float32) for _ in range(envs)]
            for t in range(shifts):
                prod = jnp.dot(lefts, diag[s + t], preferred_element_type=jnp.float32)
                prod = prod.astype(jnp.bfloat16).astype(jnp.float32)
                for e in range(envs):
                    piece = prod[:, e * side : (e + 1) * side]
                    for r in range(envs):
                        coef = table_ref[(r * envs + e) * shifts + t]
                        parts[r] = parts[r] + coef * piece
            halves = []
            rights = []
            for r in range(envs):
                high = parts[r].astype(jnp.bfloat16)
                low = (parts[r] - high.astype(jnp.float32)).astype(jnp.bfloat16)
                halves += [high, low]
                rt = stack_ref[envs + r, s]
                rights += [rt, rt]
            y = jnp.dot(
                jnp.concatenate(halves, axis=1),
                jnp.concatenate(rights, axis=0),
                preferred_element_type=jnp.float32,
            )
            image[s] = y
            x = vec[s]
            return (sums[0] + _fold(x * x), sums[1] + _fold(x * y), sums[2] + _fold(y * y))

        sx, sxy, sy = lax.fori_loop(0, sectors, apply, (zero, zero, zero), unroll=16)
        self_dot, cross_dot, image_dot = _sum_all(sx), _sum_all(sxy), _sum_all(sy)
        rayleigh_now = cross_dot / self_dot
        step_size = 0.5 * jnp.sqrt(self_dot / (image_dot + epsilon))

        keep = 1.0 + step_size * rayleigh_now
        update_sq = (
            keep * keep * self_dot
            - 2.0 * keep * step_size * cross_dot
            + step_size * step_size * image_dot
        )
        scale = lax.rsqrt(update_sq / entries + epsilon)

        def step(s, carry):
            x = vec[s]
            u = x - step_size * (image[s] - rayleigh_now * x)
            x = u * scale
            vec[s] = x
            if iteration + 1 < ITERS:
                w = x.astype(jnp.bfloat16)
                for e in range(envs):
                    diag[s + HALO, e * side : (e + 1) * side, e * side : (e + 1) * side] = w
            return carry

        lax.fori_loop(0, sectors, step, 0, unroll=4)
        cosine = cross_dot * lax.rsqrt(self_dot * (image_dot + epsilon))
    local = out_ref.shape[0]
    out_ref[...] = vec[pl.ds(place_ref[0] * local, local)]
    cos_ref[...] = jnp.broadcast_to(cosine, cos_ref.shape)


def iterate(table, place, psi, stack, local):
    _, sectors, side, _ = stack.shape
    smem = pl.BlockSpec(memory_space=pltpu.SMEM)
    vmem = pl.BlockSpec(memory_space=pltpu.VMEM)
    envs = stack.shape[0] // 2
    flops = ITERS * sectors * (2 * envs * (2 * HALO + 1) + 4 * envs) * 2 * side**3
    return pl.pallas_call(
        iterate_kernel,
        out_shape=(
            jax.ShapeDtypeStruct((local, side, side), jnp.float32),
            jax.ShapeDtypeStruct((8, 128), jnp.float32),
        ),
        in_specs=[smem, smem, vmem, vmem],
        out_specs=(vmem, vmem),
        scratch_shapes=[
            pltpu.VMEM((sectors, side, side), jnp.float32),
            pltpu.VMEM((sectors, side, side), jnp.float32),
            pltpu.VMEM((sectors + 2 * HALO, envs * side, envs * side), jnp.bfloat16),
        ],
        compiler_params=pltpu.CompilerParams(vmem_limit_bytes=48 * 1024 * 1024),
        cost_estimate=pl.CostEstimate(
            flops=flops,
            transcendentals=0,
            bytes_accessed=stack.size * 2 + 4 * local * side * side,
        ),
    )(table, place, psi, stack)


def body(
    psi_start,
    left_terms,
    left_rate,
    right_terms,
    right_rate,
    term_left,
    term_right,
    term_shift,
    term_coef,
):
    with jax.named_scope("psi_gather"):
        pair = jnp.concatenate([psi_start, psi_start], axis=0)
        psi = lax.all_gather(pair, "sector", axis=1, tiled=True)[0].astype(jnp.float32)
    with jax.named_scope("env_chain"):
        left_env, right_env = chain_envs(left_terms[0], left_rate[0], right_terms[0], right_rate[0])
    with jax.named_scope("env_gather"):
        stack = lax.all_gather(
            jnp.concatenate([left_env, jnp.swapaxes(right_env, -1, -2)], axis=0),
            "sector",
            axis=1,
            tiled=True,
        )

    envs = left_terms.shape[1]
    with jax.named_scope("term_table"):
        pick_right = (term_right[:, None] == jnp.arange(envs)[None]).astype(jnp.float32)
        pick_left = (term_left[:, None] == jnp.arange(envs)[None]).astype(jnp.float32)
        pick_shift = (term_shift[:, None] == jnp.arange(-HALO, HALO + 1)[None]).astype(jnp.float32)
        table = jnp.sum(
            term_coef[:, None, None, None]
            * pick_right[:, :, None, None]
            * pick_left[:, None, :, None]
            * pick_shift[:, None, None, :],
            axis=0,
        ).reshape(-1)
    local = psi_start.shape[1]
    place = jnp.reshape(lax.axis_index("sector"), (1,)).astype(jnp.int32)
    with jax.named_scope("iterations"):
        mine, cos = iterate(table, place, psi, stack, local)
    return (mine[None], jnp.reshape(cos[0, 0], (1,)))


def solution(mesh):
    placed = (
        P("chain", "sector", None, None),
        P("chain", None, "sector", None, None),
        P("chain", None, "sector", None),
        P("chain", None, "sector", None, None),
        P("chain", None, "sector", None),
        P(),
        P(),
        P(),
        P(),
    )
    return jax.shard_map(
        body,
        mesh=mesh,
        in_specs=placed,
        out_specs=(P("chain", "sector", None, None), P("chain")),
        check_vma=False,
    )
```

```python
import functools

import jax
import jax.numpy as jnp
from jax import lax
from jax.experimental import pallas as pl
from jax.experimental.pallas import tpu as pltpu
from jax.sharding import PartitionSpec as P

ITERS = 4
HALO = 2

epsilon = 1e-06


def chain_envs(left_terms, left_rate, right_terms, right_rate):
    count = lax.axis_size("chain")
    shape = left_terms.shape
    width = shape[-1]
    block = left_terms.size // width // count
    side = jnp.arange(2)[None, None, :, None]
    rates = jnp.where(
        side == 0, left_rate.reshape(count, 1, 1, block), right_rate.reshape(count, 1, 1, block)
    )
    part = jnp.arange(3)[None, :, None, None]
    high = lax.reduce_precision(rates, exponent_bits=8, mantissa_bits=7)
    mid = lax.reduce_precision(rates - high, exponent_bits=8, mantissa_bits=7)
    low = (rates - high) - mid
    coded = jnp.where(part == 0, high, jnp.where(part == 1, mid, low)).astype(jnp.bfloat16)
    coded = coded.reshape(count, 6 * block)
    coded = jnp.pad(coded, ((0, 0), (0, 2 * block * width - 6 * block)))
    coded = coded.reshape(count, 2 * block, width)
    packed = jnp.concatenate(
        [left_terms.reshape(count, block, width), right_terms.reshape(count, block, width), coded],
        axis=1,
    )
    spread = lax.all_to_all(packed, "chain", 0, 0, tiled=True)
    got = spread[:, 2 * block :].reshape(count, 2 * block * width)[:, : 6 * block]
    got = got.astype(jnp.float32).reshape(count, 3, 2, block)
    speed = (got[:, 0] + got[:, 1]) + got[:, 2]
    spread = spread[:, : 2 * block].astype(jnp.float32)
    ahead = jnp.cumsum(speed[:, 0], axis=0)
    behind = jnp.cumsum(speed[::-1, 1], axis=0)[::-1]
    order = jnp.arange(count)
    later = (order[:, None] >= order[None, :])[:, :, None]
    earlier = (order[:, None] <= order[None, :])[:, :, None]
    forward = jnp.where(later, ahead[:, None, :] - ahead[None, :, :], 0.0)
    backward = jnp.where(earlier, behind[:, None, :] - behind[None, :, :], 0.0)
    weight = jnp.concatenate(
        [jnp.where(later, jnp.exp(-forward), 0.0), jnp.where(earlier, jnp.exp(-backward), 0.0)],
        axis=2,
    )
    env = jnp.einsum(
        "ghp,hpc->gpc",
        weight,
        spread,
        precision=lax.Precision.HIGHEST,
        preferred_element_type=jnp.float32,
    )
    back = lax.all_to_all(env.astype(jnp.bfloat16), "chain", 0, 0, tiled=True)
    return back[:, :block].reshape(shape), back[:, block:].reshape(shape)


def _sum_all(a):
    return jnp.sum(jnp.sum(a, axis=0, keepdims=True), axis=1, keepdims=True)


def _fold(a):
    return jnp.sum(a.reshape(a.shape[0] // 8, 8, a.shape[1]), axis=0)


def iterate_kernel(table_ref, place_ref, stack_ref, out_ref, cos_ref, vec, image, diag):
    _, sectors, side, _ = stack_ref.shape
    envs = (stack_ref.shape[0] - 1) // 2
    shifts = 2 * HALO + 1
    entries = float(sectors * side * side)
    vec[...] = stack_ref[2 * envs].astype(jnp.float32)
    diag[...] = jnp.zeros(diag.shape, jnp.bfloat16)
    zero = jnp.zeros((8, side), jnp.float32)
    cosine = jnp.zeros((1, 1), jnp.float32)

    def fill(s, carry):
        w = vec[s].astype(jnp.bfloat16)
        for e in range(envs):
            diag[s + HALO, e * side : (e + 1) * side, e * side : (e + 1) * side] = w
        return carry

    lax.fori_loop(0, sectors, fill, 0)
    for iteration in range(ITERS):

        def apply(s, sums):
            lefts = jnp.concatenate([stack_ref[e, s] for e in range(envs)], axis=1)
            parts = [jnp.zeros((side, side), jnp.float32) for _ in range(envs)]
            for t in range(shifts):
                prod = jnp.dot(lefts, diag[s + t], preferred_element_type=jnp.float32)
                prod = prod.astype(jnp.bfloat16).astype(jnp.float32)
                for e in range(envs):
                    piece = prod[:, e * side : (e + 1) * side]
                    for r in range(envs):
                        coef = table_ref[(r * envs + e) * shifts + t]
                        parts[r] = parts[r] + coef * piece
            halves = []
            rights = []
            for r in range(envs):
                high = parts[r].astype(jnp.bfloat16)
                low = (parts[r] - high.astype(jnp.float32)).astype(jnp.bfloat16)
                halves += [high, low]
                rt = stack_ref[envs + r, s]
                rights += [rt, rt]
            y = jnp.dot(
                jnp.concatenate(halves, axis=1),
                jnp.concatenate(rights, axis=0),
                preferred_element_type=jnp.float32,
            )
            image[s] = y
            x = vec[s]
            return (sums[0] + _fold(x * x), sums[1] + _fold(x * y), sums[2] + _fold(y * y))

        sx, sxy, sy = lax.fori_loop(0, sectors, apply, (zero, zero, zero), unroll=16)
        self_dot, cross_dot, image_dot = _sum_all(sx), _sum_all(sxy), _sum_all(sy)
        rayleigh_now = cross_dot / self_dot
        step_size = 0.5 * jnp.sqrt(self_dot / (image_dot + epsilon))

        keep = 1.0 + step_size * rayleigh_now
        update_sq = (
            keep * keep * self_dot
            - 2.0 * keep * step_size * cross_dot
            + step_size * step_size * image_dot
        )
        scale = lax.rsqrt(update_sq / entries + epsilon)

        def step(s, carry):
            x = vec[s]
            u = x - step_size * (image[s] - rayleigh_now * x)
            x = u * scale
            vec[s] = x
            if iteration + 1 < ITERS:
                w = x.astype(jnp.bfloat16)
                for e in range(envs):
                    diag[s + HALO, e * side : (e + 1) * side, e * side : (e + 1) * side] = w
            return carry

        lax.fori_loop(0, sectors, step, 0, unroll=4)
        cosine = cross_dot * lax.rsqrt(self_dot * (image_dot + epsilon))
    local = out_ref.shape[0]
    out_ref[...] = vec[pl.ds(place_ref[0] * local, local)]
    cos_ref[...] = jnp.broadcast_to(cosine, cos_ref.shape)


def iterate(table, place, stack, local):
    _, sectors, side, _ = stack.shape
    smem = pl.BlockSpec(memory_space=pltpu.SMEM)
    vmem = pl.BlockSpec(memory_space=pltpu.VMEM)
    envs = (stack.shape[0] - 1) // 2
    flops = ITERS * sectors * (2 * envs * (2 * HALO + 1) + 4 * envs) * 2 * side**3
    return pl.pallas_call(
        iterate_kernel,
        out_shape=(
            jax.ShapeDtypeStruct((local, side, side), jnp.float32),
            jax.ShapeDtypeStruct((8, 128), jnp.float32),
        ),
        in_specs=[smem, smem, vmem],
        out_specs=(vmem, vmem),
        scratch_shapes=[
            pltpu.VMEM((sectors, side, side), jnp.float32),
            pltpu.VMEM((sectors, side, side), jnp.float32),
            pltpu.VMEM((sectors + 2 * HALO, envs * side, envs * side), jnp.bfloat16),
        ],
        compiler_params=pltpu.CompilerParams(vmem_limit_bytes=48 * 1024 * 1024),
        cost_estimate=pl.CostEstimate(
            flops=flops,
            transcendentals=0,
            bytes_accessed=stack.size * 2 + 4 * local * side * side,
        ),
    )(table, place, stack)


def body(
    psi_start,
    left_terms,
    left_rate,
    right_terms,
    right_rate,
    term_left,
    term_right,
    term_shift,
    term_coef,
):
    with jax.named_scope("env_chain"):
        left_env, right_env = chain_envs(left_terms[0], left_rate[0], right_terms[0], right_rate[0])
    with jax.named_scope("env_gather"):
        stack = lax.all_gather(
            jnp.concatenate([left_env, jnp.swapaxes(right_env, -1, -2), psi_start], axis=0),
            "sector",
            axis=1,
            tiled=True,
        )

    envs = left_terms.shape[1]
    with jax.named_scope("term_table"):
        pick_right = (term_right[:, None] == jnp.arange(envs)[None]).astype(jnp.float32)
        pick_left = (term_left[:, None] == jnp.arange(envs)[None]).astype(jnp.float32)
        pick_shift = (term_shift[:, None] == jnp.arange(-HALO, HALO + 1)[None]).astype(jnp.float32)
        table = jnp.sum(
            term_coef[:, None, None, None]
            * pick_right[:, :, None, None]
            * pick_left[:, None, :, None]
            * pick_shift[:, None, None, :],
            axis=0,
        ).reshape(-1)
    local = psi_start.shape[1]
    place = jnp.reshape(lax.axis_index("sector"), (1,)).astype(jnp.int32)
    with jax.named_scope("iterations"):
        mine, cos = iterate(table, place, stack, local)
    return (mine[None], jnp.reshape(cos[0, 0], (1,)))


def solution(mesh):
    placed = (
        P("chain", "sector", None, None),
        P("chain", None, "sector", None, None),
        P("chain", None, "sector", None),
        P("chain", None, "sector", None, None),
        P("chain", None, "sector", None),
        P(),
        P(),
        P(),
        P(),
    )
    return jax.shard_map(
        body,
        mesh=mesh,
        in_specs=placed,
        out_specs=(P("chain", "sector", None, None), P("chain")),
        check_vma=False,
    )
```

```python
import functools

import jax
import jax.numpy as jnp
from jax import lax
from jax.experimental import pallas as pl
from jax.experimental.pallas import tpu as pltpu
from jax.sharding import PartitionSpec as P

ITERS = 4
HALO = 2

epsilon = 1e-06


def chain_envs(left_terms, left_rate, right_terms, right_rate):
    count = lax.axis_size("chain")
    shape = left_terms.shape
    width = shape[-1]
    block = left_terms.size // width // count
    rates = jnp.stack([left_rate.reshape(count, block), right_rate.reshape(count, block)], axis=1)
    pieces = []
    rest = rates
    for _ in range(3):
        piece = lax.reduce_precision(rest, exponent_bits=8, mantissa_bits=7)
        rest = rest - piece
        pieces.append(piece.astype(jnp.bfloat16))
    coded = jnp.stack(pieces, axis=1).reshape(count, 6 * block)
    coded = jnp.pad(coded, ((0, 0), (0, 2 * block * width - 6 * block)))
    coded = coded.reshape(count, 2 * block, width)
    packed = jnp.concatenate(
        [left_terms.reshape(count, block, width), right_terms.reshape(count, block, width), coded],
        axis=1,
    )
    spread = lax.all_to_all(packed, "chain", 0, 0, tiled=True)
    got = spread[:, 2 * block :].reshape(count, 2 * block * width)[:, : 6 * block]
    got = got.astype(jnp.float32).reshape(count, 3, 2, block)
    speed = (got[:, 0] + got[:, 1]) + got[:, 2]
    spread = spread[:, : 2 * block].astype(jnp.float32)
    ahead = jnp.cumsum(speed[:, 0], axis=0)
    behind = jnp.cumsum(speed[::-1, 1], axis=0)[::-1]
    order = jnp.arange(count)
    later = (order[:, None] >= order[None, :])[:, :, None]
    earlier = (order[:, None] <= order[None, :])[:, :, None]
    forward = jnp.where(later, ahead[:, None, :] - ahead[None, :, :], 0.0)
    backward = jnp.where(earlier, behind[:, None, :] - behind[None, :, :], 0.0)
    weight = jnp.concatenate(
        [jnp.where(later, jnp.exp(-forward), 0.0), jnp.where(earlier, jnp.exp(-backward), 0.0)],
        axis=2,
    )
    env = jnp.einsum(
        "ghp,hpc->gpc",
        weight,
        spread,
        precision=lax.Precision.HIGHEST,
        preferred_element_type=jnp.float32,
    )
    back = lax.all_to_all(env.astype(jnp.bfloat16), "chain", 0, 0, tiled=True)
    return back[:, :block].reshape(shape), back[:, block:].reshape(shape)


def _sum_all(a):
    return jnp.sum(jnp.sum(a, axis=0, keepdims=True), axis=1, keepdims=True)


def _fold(a):
    return jnp.sum(a.reshape(a.shape[0] // 8, 8, a.shape[1]), axis=0)


def iterate_kernel(table_ref, place_ref, stack_ref, out_ref, cos_ref, vec, image, diag):
    _, sectors, side, _ = stack_ref.shape
    envs = (stack_ref.shape[0] - 1) // 2
    shifts = 2 * HALO + 1
    entries = float(sectors * side * side)
    vec[...] = stack_ref[2 * envs].astype(jnp.float32)
    block = jnp.zeros((diag.shape[0], side, side), jnp.bfloat16)
    for e in range(envs):
        for f in range(envs):
            if e != f:
                diag[:, e * side : (e + 1) * side, f * side : (f + 1) * side] = block
    rim = jnp.zeros((HALO,) + diag.shape[1:], jnp.bfloat16)
    diag[0:HALO] = rim
    diag[HALO + sectors : 2 * HALO + sectors] = rim
    zero = jnp.zeros((8, side), jnp.float32)
    cosine = jnp.zeros((1, 1), jnp.float32)

    def fill(s, carry):
        w = vec[s].astype(jnp.bfloat16)
        for e in range(envs):
            diag[s + HALO, e * side : (e + 1) * side, e * side : (e + 1) * side] = w
        return carry

    lax.fori_loop(0, sectors, fill, 0, unroll=True)
    for iteration in range(ITERS):

        def apply(s, sums):
            lefts = jnp.concatenate([stack_ref[e, s] for e in range(envs)], axis=1)
            parts = [jnp.zeros((side, side), jnp.float32) for _ in range(envs)]
            for t in range(shifts):
                prod = jnp.dot(lefts, diag[s + t], preferred_element_type=jnp.float32)
                prod = prod.astype(jnp.bfloat16).astype(jnp.float32)
                for e in range(envs):
                    piece = prod[:, e * side : (e + 1) * side]
                    for r in range(envs):
                        coef = table_ref[(r * envs + e) * shifts + t]
                        parts[r] = parts[r] + coef * piece
            halves = []
            rights = []
            for r in range(envs):
                high = parts[r].astype(jnp.bfloat16)
                low = (parts[r] - high.astype(jnp.float32)).astype(jnp.bfloat16)
                halves += [high, low]
                rt = stack_ref[envs + r, s]
                rights += [rt, rt]
            y = jnp.dot(
                jnp.concatenate(halves, axis=1),
                jnp.concatenate(rights, axis=0),
                preferred_element_type=jnp.float32,
            )
            image[s] = y
            x = vec[s]
            return (sums[0] + _fold(x * x), sums[1] + _fold(x * y), sums[2] + _fold(y * y))

        sx, sxy, sy = lax.fori_loop(0, sectors, apply, (zero, zero, zero), unroll=16)
        self_dot, cross_dot, image_dot = _sum_all(sx), _sum_all(sxy), _sum_all(sy)
        rayleigh_now = cross_dot / self_dot
        step_size = 0.5 * jnp.sqrt(self_dot / (image_dot + epsilon))

        keep = 1.0 + step_size * rayleigh_now
        update_sq = (
            keep * keep * self_dot
            - 2.0 * keep * step_size * cross_dot
            + step_size * step_size * image_dot
        )
        scale = lax.rsqrt(update_sq / entries + epsilon)

        def step(s, carry):
            x = vec[s]
            u = x - step_size * (image[s] - rayleigh_now * x)
            x = u * scale
            vec[s] = x
            if iteration + 1 < ITERS:
                w = x.astype(jnp.bfloat16)
                for e in range(envs):
                    diag[s + HALO, e * side : (e + 1) * side, e * side : (e + 1) * side] = w
            return carry

        lax.fori_loop(0, sectors, step, 0, unroll=True)
        cosine = cross_dot * lax.rsqrt(self_dot * (image_dot + epsilon))
    local = out_ref.shape[0]
    out_ref[...] = vec[pl.ds(place_ref[0] * local, local)]
    cos_ref[...] = jnp.broadcast_to(cosine, cos_ref.shape)


def iterate(table, place, stack, local):
    _, sectors, side, _ = stack.shape
    smem = pl.BlockSpec(memory_space=pltpu.SMEM)
    vmem = pl.BlockSpec(memory_space=pltpu.VMEM)
    envs = (stack.shape[0] - 1) // 2
    flops = ITERS * sectors * (2 * envs * (2 * HALO + 1) + 4 * envs) * 2 * side**3
    return pl.pallas_call(
        iterate_kernel,
        out_shape=(
            jax.ShapeDtypeStruct((local, side, side), jnp.float32),
            jax.ShapeDtypeStruct((8, 128), jnp.float32),
        ),
        in_specs=[smem, smem, vmem],
        out_specs=(vmem, vmem),
        scratch_shapes=[
            pltpu.VMEM((sectors, side, side), jnp.float32),
            pltpu.VMEM((sectors, side, side), jnp.float32),
            pltpu.VMEM((sectors + 2 * HALO, envs * side, envs * side), jnp.bfloat16),
        ],
        compiler_params=pltpu.CompilerParams(vmem_limit_bytes=48 * 1024 * 1024),
        cost_estimate=pl.CostEstimate(
            flops=flops,
            transcendentals=0,
            bytes_accessed=stack.size * 2 + 4 * local * side * side,
        ),
    )(table, place, stack)


def body(
    psi_start,
    left_terms,
    left_rate,
    right_terms,
    right_rate,
    term_left,
    term_right,
    term_shift,
    term_coef,
):
    with jax.named_scope("env_chain"):
        left_env, right_env = chain_envs(left_terms[0], left_rate[0], right_terms[0], right_rate[0])
    with jax.named_scope("env_gather"):
        stack = lax.all_gather(
            jnp.concatenate([left_env, jnp.swapaxes(right_env, -1, -2), psi_start], axis=0),
            "sector",
            axis=1,
            tiled=True,
        )

    envs = left_terms.shape[1]
    with jax.named_scope("term_table"):
        pick_right = (term_right[:, None] == jnp.arange(envs)[None]).astype(jnp.float32)
        pick_left = (term_left[:, None] == jnp.arange(envs)[None]).astype(jnp.float32)
        pick_shift = (term_shift[:, None] == jnp.arange(-HALO, HALO + 1)[None]).astype(jnp.float32)
        table = jnp.sum(
            term_coef[:, None, None, None]
            * pick_right[:, :, None, None]
            * pick_left[:, None, :, None]
            * pick_shift[:, None, None, :],
            axis=0,
        ).reshape(-1)
    local = psi_start.shape[1]
    place = jnp.reshape(lax.axis_index("sector"), (1,)).astype(jnp.int32)
    with jax.named_scope("iterations"):
        mine, cos = iterate(table, place, stack, local)
    return (mine[None], jnp.reshape(cos[0, 0], (1,)))


def solution(mesh):
    placed = (
        P("chain", "sector", None, None),
        P("chain", None, "sector", None, None),
        P("chain", None, "sector", None),
        P("chain", None, "sector", None, None),
        P("chain", None, "sector", None),
        P(),
        P(),
        P(),
        P(),
    )
    return jax.shard_map(
        body,
        mesh=mesh,
        in_specs=placed,
        out_specs=(P("chain", "sector", None, None), P("chain")),
        check_vma=False,
    )
```
